32 devices in a mesh: row: 4 (over z), col: 8 (over y, x, core).
Axes of the slice: x: 2, y: 2, z: 4, core: 2. Of those that a mesh axis runs over, the one named last changes fastest.
Arguments:
- tokens: bfloat16 [12288, 1024], P(('row', 'col')), may hold values from -6 to 6
- segment_ids: int32 [32, 384], P(('row', 'col')), may hold values from 0 to 3, never falling along the last dimension, each value on 1 to 192 neighbouring positions
- gain_in: float32 [1024], replicated, may hold values from 0.5 to 1.5
- w_qkv: bfloat16 [1024, 3072], replicated, may hold values from -0.1875 to 0.1875
- conv_w: float32 [4, 3072], replicated, may hold values from -3 to 3
- w_decay: bfloat16 [1024, 12], replicated, may hold values from -0.1875 to 0.1875
- a_log: float32 [6], replicated, may hold values from -7 to -2.5
- dt_bias: float32 [6], replicated, may hold values from -3 to 3
- w_gate_o: bfloat16 [1024, 1536], replicated, may hold values from -0.1875 to 0.1875
- gain_o: float32 [256], replicated, may hold values from 0.5 to 1.5
- w_out: bfloat16 [1536, 1024], replicated, may hold values from -0.3125 to 0.3125
- gain_mid: float32 [1024], replicated, may hold values from 0.5 to 1.5
- w_gate_up: bfloat16 [2, 1024, 2816], P(None, 'row', 'col'), may hold values from -0.1875 to 0.1875
- w_down: bfloat16 [2816, 1024], P('col', 'row'), may hold values from -0.109375 to 0.109375
- cotangent: bfloat16 [12288, 1024], P(('row', 'col')), may hold values from -6 to 6
Outputs:
- block_out: bfloat16 [12288, 1024], P(('row', 'col'))
- grad_tokens: float32 [12288, 1024], P(('row', 'col'))
- grad_gain_in: float32 [1024], replicated
- grad_qkv: float32 [1024, 3072], replicated
- grad_conv: float32 [4, 3072], replicated
- grad_decay: float32 [1024, 12], replicated
- grad_a_log: float32 [6], replicated
- grad_dt_bias: float32 [6], replicated
- grad_gate_o: float32 [1024, 1536], replicated
- grad_gain_o: float32 [256], replicated
- grad_out: float32 [1536, 1024], replicated
- grad_gain_mid: float32 [1024], replicated
- grad_gate_up: float32 [2, 1024, 2816], P(None, 'row', 'col')
- grad_down: float32 [2816, 1024], P('col', 'row')
The draws below stay inside these ranges and needn't reach their ends.
Inputs may be any that keep to these rules, and one draw needn't show every extreme that they name: Each row of segment_ids (one device's 384 tokens) holds whole sequences: the numbers never fall along the row, and a sequence spans 1 to 192 positions.
All inputs are finite; a program needn't handle non-finite values.
Results may differ from the reference program's by a relative error of at most 0.015.
The reference program's roundings to bfloat16 on the way (of `normed_in`, `mixed`, `normed_mid`, `hidden`, `grad_gate_pre` and `grad_middle_b`) count: a program that leaves them out, or rounds other values in their place, can miss the bound.
Values may be sent and summed in bfloat16 or wider, within the bound.
No kernel may reach another device: no remote copies, remote signals or barrier semaphores. Data moves between devices by JAX's collectives and lax.ppermute only.
A program may use at most 384 MiB of HBM per device.

```python
import math
import jax
import jax.numpy as jnp
import numpy as np
from jax import lax

D = 1024
HEADS = 6
HEAD_K = 128
HEAD_V = 256
FF = 2816
CONV = 4
STRETCH = 64
SEQS = 4
TOK_DEV = 384
SEG_MOST = 192
TOKENS = 12288
VALUE_DIM = 1536
QKV = 3072
N_ROW = 4
N_COL = 8


def level_of(own_key, shape, cuts, least, high):
    gain = 1.0
    for axis_at, parts in cuts:
        steps = jax.random.uniform(jax.random.fold_in(jax.random.fold_in(own_key, 6), axis_at), (parts,), jnp.float32, least / len(cuts), high / len(cuts))
        gain = gain * jnp.repeat(jnp.exp(steps), shape[axis_at] // parts).reshape((-1,) + (1,) * (len(shape) - 1 - axis_at))
    return gain


def split_up(count, total, bound, skew):
    weights = [(1 << 20) // math.isqrt(grade ** skew) + 1 for grade in range(2, count + 1)]
    spare, counts = total - bound - (count - 1), [1] * (count - 1)
    while spare > 0:
        movable = [i for i in range(count - 1) if counts[i] < bound]
        mass, budget = sum([weights[i] for i in movable]), spare
        for i in movable:
            extra = min(bound - counts[i], max(1, budget * weights[i] // mass), spare)
            counts[i] = counts[i] + extra
            spare = spare - extra
    return np.array([bound] + counts)


def uneven_parts(stream_key, count, total, limit, lean):
    if count == 2:
        one = jax.random.randint(stream_key, (), max(1, total - limit), min(limit, total - 1) + 1)
        return jnp.stack([one, total - one])
    sizes = jnp.asarray(split_up(count, total, limit, lean), jnp.int32)
    pairs = (count - 1) // 2
    donor, receiver = sizes[1:1 + 2 * pairs:2], sizes[2:2 + 2 * pairs:2]
    room = jnp.minimum(donor - 1, limit - receiver)
    passed = jax.random.randint(jax.random.fold_in(stream_key, 1), (pairs,), 0, 1 << 20) % (room + 1)
    sizes = sizes.at[1:1 + 2 * pairs:2].set(donor - passed).at[2:2 + 2 * pairs:2].set(receiver + passed)
    return sizes[jax.random.permutation(jax.random.fold_in(stream_key, 2), count)]


def gaussian(stream_key, extent, scale, most, cuts=(), kind=jnp.bfloat16):
    values = jax.random.normal(stream_key, extent, jnp.float32) * scale
    if len(cuts) > 0:
        values = level_of(stream_key, extent, cuts, -0.22, 0.18) * values
    return jnp.clip(values, min=-most, max=most).astype(kind)


def setup_inputs(seed: int = 0) -> dict:
    arg_keys = jax.random.split(jax.random.key(seed), 16)
    tokens = gaussian(arg_keys[0], (TOKENS, D), 1.0, 6.0, ((0, 32),))
    segment_ids = jax.vmap(lambda own: jnp.searchsorted(jnp.cumsum(uneven_parts(own, SEQS, TOK_DEV, SEG_MOST, 2)), jnp.arange(TOK_DEV), side="right"))(jax.random.split(arg_keys[1], (N_ROW * N_COL))).reshape((N_ROW * N_COL, TOK_DEV)).astype(jnp.int32)
    gain_in = jnp.clip(1.0 + 0.1 * jax.random.normal(arg_keys[2], (D,), jnp.float32), 0.5, 1.5)
    w_qkv = gaussian(arg_keys[3], (D, QKV), D ** -0.5, 0.1875)
    conv_w = gaussian(arg_keys[4], (CONV, QKV), 0.5, 3.0, (), jnp.float32)
    w_decay = gaussian(arg_keys[5], (D, 2 * HEADS), D ** -0.5, 0.1875)
    a_log = jnp.clip(jax.random.uniform(arg_keys[6], (HEADS,), jnp.float32, -7.0, -2.5), -7.0, -2.5)
    dt_bias = gaussian(arg_keys[7], (HEADS,), 1.0, 3.0, (), jnp.float32)
    w_gate_o = gaussian(arg_keys[8], (D, VALUE_DIM), D ** -0.5, 0.1875)
    gain_o = jnp.clip(1.0 + 0.1 * jax.random.normal(arg_keys[9], (HEAD_V,), jnp.float32), 0.5, 1.5)
    w_out = gaussian(arg_keys[10], (VALUE_DIM, D), (VALUE_DIM // 4) ** -0.5, 0.3125)
    gain_mid = jnp.clip(1.0 + 0.1 * jax.random.normal(arg_keys[11], (D,), jnp.float32), 0.5, 1.5)
    w_gate_up = gaussian(arg_keys[12], (2, D, FF), D ** -0.5, 0.1875, ((1, 4), (2, 8)))
    w_down = gaussian(arg_keys[13], (FF, D), FF ** -0.5, 0.109375, ((0, 8), (1, 4)))
    cotangent = gaussian(arg_keys[14], (TOKENS, D), 1.0, 6.0, ((0, 32),))
    return {"tokens": tokens, "segment_ids": segment_ids, "gain_in": gain_in, "w_qkv": w_qkv, "conv_w": conv_w, "w_decay": w_decay, "a_log": a_log, "dt_bias": dt_bias, "w_gate_o": w_gate_o, "gain_o": gain_o, "w_out": w_out, "gain_mid": gain_mid, "w_gate_up": w_gate_up, "w_down": w_down, "cotangent": cotangent}


EPSILON = 1e-06

def rms_scale(values, gain_vec):
    return values * lax.rsqrt(lax.optimization_barrier(jnp.mean(values * values, axis=-1, keepdims=True)) + EPSILON) * gain_vec

def conv_silu(raw_proj, conv_weight, segments):
    length = raw_proj.shape[0]
    mixed = raw_proj * conv_weight[CONV - 1]
    for offset in range(1, CONV):
        shifted = jnp.concatenate([jnp.zeros((offset, raw_proj.shape[1]), jnp.float32), raw_proj[:length - offset]], axis=0)
        seg_shifted = jnp.concatenate([jnp.full((offset,), -1, jnp.int32), segments[:length - offset]], axis=0)
        keep_tap = (seg_shifted == segments).astype(jnp.float32)[:, None]
        mixed = mixed + shifted * keep_tap * conv_weight[CONV - 1 - offset]
    return jax.nn.silu(mixed)

def head_blocks(array, stretch_count):
    shaped = array.reshape((stretch_count, STRETCH) + array.shape[1:])
    return jnp.swapaxes(shaped, 1, 2)

def delta_rule(queries, keys_unit, values_part, log_decay, write_rate, segments):
    length = queries.shape[0]
    stretch_count = length // STRETCH
    highest_precision = lax.Precision.HIGHEST
    seg_blocks = segments.reshape(stretch_count, STRETCH)
    seg_before = jnp.concatenate([jnp.full((1,), -1, jnp.int32), seg_blocks[:-1, -1]], axis=0)
    row_index = jnp.arange(STRETCH)[:, None]
    col_index = jnp.arange(STRETCH)[None, :]
    identity = jnp.eye(STRETCH, dtype=jnp.float32)

    def stretch_step(key_value_state, inputs):
        query_segment, key_segment, value_c, decay_c, rate_c, seg_c, seg_prev = inputs
        cumulative = jnp.cumsum(decay_c, axis=-1)
        live = (seg_c[:, None] == seg_c[None, :]) & (row_index >= col_index)
        gap_log = cumulative[:, :, None] - cumulative[:, None, :]
        decay_mat = jnp.where(live[None], jnp.exp(jnp.where(live[None], gap_log, 0.0)), 0.0)
        incoming_carry = jnp.exp(cumulative) * (seg_c == seg_prev).astype(jnp.float32)[None, :]
        key_gram = jnp.einsum('hck,hsk->hcs', key_segment, key_segment, precision=highest_precision)
        strict = jnp.where((row_index > col_index)[None], decay_mat, 0.0)
        lower_mat = identity[None] + rate_c[:, :, None] * strict * key_gram
        state_contribution = jnp.einsum('jlf,jfs->jls', key_segment, key_value_state, precision=highest_precision)
        right_side = rate_c[:, :, None] * (value_c - incoming_carry[:, :, None] * state_contribution)
        pseudo_target = jax.scipy.linalg.solve_triangular(lower_mat, right_side, lower=True)
        scores = jnp.einsum('hck,hsk->hcs', query_segment, key_segment, precision=highest_precision) * decay_mat
        output_rows = incoming_carry[:, :, None] * jnp.einsum('jlf,jfs->jls', query_segment, key_value_state, precision=highest_precision)
        output_rows = output_rows + jnp.einsum('hcs,hsv->hcv', scores, pseudo_target, precision=highest_precision)
        weighted_values = key_segment * decay_mat[:, -1, :, None]
        updated_state = incoming_carry[:, -1][:, None, None] * key_value_state + jnp.einsum('gub,gue->gbe', weighted_values, pseudo_target, precision=highest_precision)
        return (updated_state, output_rows)
    initial = jnp.zeros((HEADS, HEAD_K, HEAD_V), jnp.float32)
    inputs = (head_blocks(queries, stretch_count), head_blocks(keys_unit, stretch_count), head_blocks(values_part, stretch_count), head_blocks(log_decay, stretch_count), head_blocks(write_rate, stretch_count), seg_blocks, seg_before)
    _, stacked = lax.scan(stretch_step, initial, inputs)
    return jnp.swapaxes(stacked, 1, 2).reshape(length, HEADS, HEAD_V)

def mixer(raw_proj, gate_logits, out_gate, segments, conv_weight, a_log, dt_bias, gain_o):
    length = raw_proj.shape[0]
    key_dim = HEADS * HEAD_K
    conv = conv_silu(raw_proj, conv_weight, segments)
    queries = conv[:, :key_dim].reshape(length, HEADS, HEAD_K)
    keys_raw = conv[:, key_dim:2 * key_dim].reshape(length, HEADS, HEAD_K)
    values_part = conv[:, 2 * key_dim:].reshape(length, HEADS, HEAD_V)
    queries = queries * lax.rsqrt(lax.optimization_barrier(jnp.sum(queries * queries, axis=-1, keepdims=True)) + EPSILON) * HEAD_K ** (-0.5)
    keys_unit = keys_raw * lax.rsqrt(lax.optimization_barrier(jnp.sum(keys_raw * keys_raw, axis=-1, keepdims=True)) + EPSILON)
    log_decay = -jnp.exp(a_log) * jax.nn.softplus(gate_logits[:, :HEADS] + dt_bias)
    write_rate = jax.nn.sigmoid(gate_logits[:, HEADS:])
    delta_out = delta_rule(queries, keys_unit, values_part, log_decay, write_rate, segments)
    gate_vals = jax.nn.silu(out_gate).reshape(length, HEADS, HEAD_V)
    normed = delta_out * lax.rsqrt(lax.optimization_barrier(jnp.mean(delta_out * delta_out, axis=-1, keepdims=True)) + EPSILON) * gain_o * gate_vals
    return normed.reshape(length, HEADS * HEAD_V)

def contract_rows(left, right):
    return lax.dot_general(left.astype(jnp.float32), right.astype(jnp.float32), (((0,), (0,)), ((), ())), preferred_element_type=jnp.float32)

def contract_cols(left, right):
    return lax.dot_general(left.astype(jnp.float32), right.astype(jnp.float32), (((1,), (1,)), ((), ())), preferred_element_type=jnp.float32)

def layer_block(tok_block, segments, cot_block, params):
    gain_in, w_qkv, conv_w, w_decay, a_log, dt_bias, w_gate_o, gain_o, w_out, gain_mid, w_gate_up, w_down = params
    residual_in = tok_block.astype(jnp.float32)
    normed_f, norm_in_back = jax.vjp(rms_scale, residual_in, gain_in)
    normed_in = normed_f.astype(jnp.bfloat16)
    raw_proj = jnp.dot(normed_in.astype(jnp.float32), w_qkv.astype(jnp.float32), preferred_element_type=jnp.float32)
    gate_logits = jnp.dot(normed_in.astype(jnp.float32), w_decay.astype(jnp.float32), preferred_element_type=jnp.float32)
    out_gate = jnp.dot(normed_in.astype(jnp.float32), w_gate_o.astype(jnp.float32), preferred_element_type=jnp.float32)

    def local_mixer(raw_a, logit_a, gate_a, conv_a, log_a, bias_a, gain_a):
        return mixer(raw_a, logit_a, gate_a, segments, conv_a, log_a, bias_a, gain_a)
    mixed_f, mixer_back = jax.vjp(local_mixer, raw_proj, gate_logits, out_gate, conv_w, a_log, dt_bias, gain_o)
    mixed = mixed_f.astype(jnp.bfloat16)
    middle = residual_in + jnp.dot(mixed.astype(jnp.float32), w_out.astype(jnp.float32), preferred_element_type=jnp.float32)
    normed_mf, norm_mid_back = jax.vjp(rms_scale, middle, gain_mid)
    normed_mid = normed_mf.astype(jnp.bfloat16)
    gate_pre = jnp.dot(normed_mid.astype(jnp.float32), w_gate_up[0].astype(jnp.float32), preferred_element_type=jnp.float32)
    up_proj = jnp.dot(normed_mid.astype(jnp.float32), w_gate_up[1].astype(jnp.float32), preferred_element_type=jnp.float32)
    hidden = (jax.nn.silu(gate_pre) * up_proj).astype(jnp.bfloat16)
    block_out = (middle + jnp.dot(hidden.astype(jnp.float32), w_down.astype(jnp.float32), preferred_element_type=jnp.float32)).astype(jnp.bfloat16)
    grad_hidden = contract_cols(cot_block, w_down)
    sigmoid_g = jax.nn.sigmoid(gate_pre)
    grad_gate_pre = (grad_hidden * up_proj * sigmoid_g * (1.0 + gate_pre * (1.0 - sigmoid_g))).astype(jnp.bfloat16)
    grad_up = (grad_hidden * gate_pre * sigmoid_g).astype(jnp.bfloat16)
    grad_down = contract_rows(hidden, cot_block)
    grad_gate_up = jnp.stack([contract_rows(normed_mid, grad_gate_pre), contract_rows(normed_mid, grad_up)])
    grad_normed_mid = contract_cols(grad_gate_pre, w_gate_up[0]) + contract_cols(grad_up, w_gate_up[1])
    grad_mid_norm, grad_gain_mid = norm_mid_back(grad_normed_mid)
    grad_middle = cot_block.astype(jnp.float32) + grad_mid_norm
    grad_middle_b = grad_middle.astype(jnp.bfloat16)
    grad_out = contract_rows(mixed, grad_middle_b)
    grad_mixed = contract_cols(grad_middle_b, w_out)
    grad_raw, grad_logits, grad_gate_out, grad_conv, grad_a_log, grad_dt_bias, grad_gain_o = mixer_back(grad_mixed)
    grad_raw_b = grad_raw.astype(jnp.bfloat16)
    grad_logits_b = grad_logits.astype(jnp.bfloat16)
    grad_gate_b = grad_gate_out.astype(jnp.bfloat16)
    grad_qkv = contract_rows(normed_in, grad_raw_b)
    grad_decay = contract_rows(normed_in, grad_logits_b)
    grad_gate_o = contract_rows(normed_in, grad_gate_b)
    grad_normed_in = contract_cols(grad_raw_b, w_qkv) + contract_cols(grad_logits_b, w_decay) + contract_cols(grad_gate_b, w_gate_o)
    grad_in_norm, grad_gain_in = norm_in_back(grad_normed_in)
    grad_tokens = grad_middle + grad_in_norm
    grads = (grad_gain_in, grad_qkv, grad_conv, grad_decay, grad_a_log, grad_dt_bias, grad_gate_o, grad_gain_o, grad_out, grad_gain_mid, grad_gate_up, grad_down)
    return (block_out, grad_tokens, grads)

def reference(tokens, segment_ids, gain_in, w_qkv, conv_w, w_decay, a_log, dt_bias, w_gate_o, gain_o, w_out, gain_mid, w_gate_up, w_down, cotangent):
    block_count = segment_ids.shape[0]
    params = (gain_in, w_qkv, conv_w, w_decay, a_log, dt_bias, w_gate_o, gain_o, w_out, gain_mid, w_gate_up, w_down)
    zero_grads = tuple((jnp.zeros(param_arr.shape, jnp.float32) for param_arr in params))
    token_blocks = tokens.reshape(block_count, TOK_DEV, D)
    cot_blocks = cotangent.reshape(block_count, TOK_DEV, D)

    def scan_step(totals, inputs):
        tok_block, seg_block, cot_block = inputs
        out_block, grad_block, grads = layer_block(tok_block, seg_block, cot_block, params)
        return (tuple((total_g + part_g for total_g, part_g in zip(totals, grads))), (out_block, grad_block))
    totals, (out_rows, grad_rows) = lax.scan(scan_step, zero_grads, (token_blocks, segment_ids, cot_blocks))
    return (out_rows.reshape(block_count * TOK_DEV, D), grad_rows.reshape(block_count * TOK_DEV, D), totals[0], totals[1], totals[2], totals[3], totals[4], totals[5], totals[6], totals[7], totals[8], totals[9], totals[10], totals[11])
```

```python
import jax
import jax.numpy as jnp
from jax import lax
from jax.sharding import PartitionSpec as P

HEADS = 6
HEAD_K = 128
HEAD_V = 256
CONV = 4
STRETCH = 64
HI = lax.Precision.HIGHEST


EPSILON = 1e-06


def rms_scale(values, gain_vec):
    return (
        values * lax.rsqrt(jnp.mean(values * values, axis=-1, keepdims=True) + EPSILON) * gain_vec
    )


def conv_silu(raw_proj, conv_weight, segments):
    length = raw_proj.shape[0]
    mixed = raw_proj * conv_weight[CONV - 1]
    for offset in range(1, CONV):
        shifted = jnp.concatenate(
            [jnp.zeros((offset, raw_proj.shape[1]), jnp.float32), raw_proj[: length - offset]],
            axis=0,
        )
        seg_shifted = jnp.concatenate(
            [jnp.full((offset,), -1, jnp.int32), segments[: length - offset]], axis=0
        )
        keep_tap = (seg_shifted == segments).astype(jnp.float32)[:, None]
        mixed = mixed + shifted * keep_tap * conv_weight[CONV - 1 - offset]
    return jax.nn.silu(mixed)


def head_blocks(array, stretch_count):
    shaped = array.reshape((stretch_count, STRETCH) + array.shape[1:])
    return jnp.swapaxes(shaped, 1, 2)


LEAF = 8


def _mm(a, b):
    return jnp.einsum("...ij,...jk->...ik", a, b, precision=HI)


def _unit_lower_inverse_fwd_impl(strict_part):
    n = strict_part.shape[-1]
    lead = strict_part.shape[:-2]
    nb = n // LEAF
    eye = jnp.eye(LEAF, dtype=strict_part.dtype)
    diag = jnp.stack(
        [strict_part[..., i * LEAF:(i + 1) * LEAF, i * LEAF:(i + 1) * LEAF] for i in range(nb)], axis=-3
    )
    sq = _mm(diag, diag)
    blocks = _mm(_mm(eye - diag, eye + sq), eye + _mm(sq, sq))
    size = LEAF
    while size < n:
        count = n // (2 * size)
        upper_inv = blocks[..., 0::2, :, :]
        lower_inv = blocks[..., 1::2, :, :]
        cross = jnp.stack(
            [strict_part[..., (2 * p + 1) * size:(2 * p + 2) * size, 2 * p * size:(2 * p + 1) * size] for p in range(count)],
            axis=-3,
        )
        corner = -_mm(lower_inv, _mm(cross, upper_inv))
        zeros = jnp.zeros_like(corner)
        top = jnp.concatenate([upper_inv, zeros], axis=-1)
        bottom = jnp.concatenate([corner, lower_inv], axis=-1)
        blocks = jnp.concatenate([top, bottom], axis=-2)
        size *= 2
    return blocks[..., 0, :, :]


@jax.custom_vjp
def unit_lower_inverse(strict_part):
    return _unit_lower_inverse_fwd_impl(strict_part)


def _uli_fwd(strict_part):
    inv = _unit_lower_inverse_fwd_impl(strict_part)
    return inv, inv


def _uli_bwd(inv, grad):
    n = inv.shape[-1]
    below = jnp.arange(n)[:, None] > jnp.arange(n)[None, :]
    inv_t = jnp.swapaxes(inv, -1, -2)
    return (jnp.where(below, -_mm(inv_t, _mm(grad, inv_t)), 0.0),)


unit_lower_inverse.defvjp(_uli_fwd, _uli_bwd)


def delta_rule(queries, keys_unit, values_part, log_decay, write_rate, segments):
    length = queries.shape[0]
    nc = length // STRETCH
    q = head_blocks(queries, nc)
    k = head_blocks(keys_unit, nc)
    v = head_blocks(values_part, nc)
    g = head_blocks(log_decay, nc)
    beta = head_blocks(write_rate, nc)
    seg = segments.reshape(nc, STRETCH)
    seg_prev = jnp.concatenate([jnp.full((1,), -1, jnp.int32), seg[:-1, -1]], axis=0)
    row = jnp.arange(STRETCH)[:, None]
    col = jnp.arange(STRETCH)[None, :]
    cum = jnp.cumsum(g, axis=-1)
    live = ((seg[:, :, None] == seg[:, None, :]) & (row >= col))[:, None]
    gap = cum[..., :, None] - cum[..., None, :]
    decay_mat = jnp.where(live, jnp.exp(jnp.where(live, gap, 0.0)), 0.0)
    carry = jnp.exp(cum) * (seg == seg_prev[:, None]).astype(jnp.float32)[:, None, :]
    gram = jnp.einsum("nhck,nhsk->nhcs", k, k, precision=HI)
    strict = jnp.where((row > col)[None, None], decay_mat, 0.0)
    inverse = unit_lower_inverse(beta[..., None] * strict * gram)
    rhs = jnp.concatenate([beta[..., None] * v, (beta * carry)[..., None] * k], axis=-1)
    sol = jnp.einsum("nhcs,nhsv->nhcv", inverse, rhs, precision=HI)
    u, w = sol[..., :HEAD_V], sol[..., HEAD_V:]
    kw = k * decay_mat[..., -1, :, None]
    m = jnp.einsum("nhck,nhcj->nhkj", kw, w, precision=HI)
    nn = jnp.einsum("nhck,nhcv->nhkv", kw, u, precision=HI)
    a_last = carry[..., -1]
    states = [jnp.zeros((HEADS, HEAD_K, HEAD_V), jnp.float32)]
    s = nn[0]
    states.append(s)
    for c in range(1, nc - 1):
        s = a_last[c][:, None, None] * s - jnp.einsum("hkj,hjv->hkv", m[c], s, precision=HI) + nn[c]
        states.append(s)
    st = jnp.stack(states)
    p = u - jnp.einsum("nhck,nhkv->nhcv", w, st, precision=HI)
    scores = jnp.einsum("nhck,nhsk->nhcs", q, k, precision=HI) * decay_mat
    out = carry[..., None] * jnp.einsum("nhck,nhkv->nhcv", q, st, precision=HI)
    out = out + jnp.einsum("nhcs,nhsv->nhcv", scores, p, precision=HI)
    return jnp.swapaxes(out, 1, 2).reshape(length, HEADS, HEAD_V)


def mixer(raw_proj, gate_logits, out_gate, segments, conv_weight, a_log, dt_bias, gain_o):
    length = raw_proj.shape[0]
    key_dim = HEADS * HEAD_K
    conv = conv_silu(raw_proj, conv_weight, segments)
    queries = conv[:, :key_dim].reshape(length, HEADS, HEAD_K)
    keys_raw = conv[:, key_dim : 2 * key_dim].reshape(length, HEADS, HEAD_K)
    values_part = conv[:, 2 * key_dim :].reshape(length, HEADS, HEAD_V)
    queries = (
        queries
        * lax.rsqrt(jnp.sum(queries * queries, axis=-1, keepdims=True) + EPSILON)
        * HEAD_K ** (-0.5)
    )
    keys_unit = keys_raw * lax.rsqrt(jnp.sum(keys_raw * keys_raw, axis=-1, keepdims=True) + EPSILON)
    log_decay = -jnp.exp(a_log) * jax.nn.softplus(gate_logits[:, :HEADS] + dt_bias)
    write_rate = jax.nn.sigmoid(gate_logits[:, HEADS:])
    delta_out = delta_rule(queries, keys_unit, values_part, log_decay, write_rate, segments)
    gate_vals = jax.nn.silu(out_gate).reshape(length, HEADS, HEAD_V)
    normed = (
        delta_out
        * lax.rsqrt(jnp.mean(delta_out * delta_out, axis=-1, keepdims=True) + EPSILON)
        * gain_o
        * gate_vals
    )
    return normed.reshape(length, HEADS * HEAD_V)


def contract_rows(left, right):
    return lax.dot_general(
        left, right, (((0,), (0,)), ((), ())), preferred_element_type=jnp.float32
    )


def contract_cols(left, right):
    return lax.dot_general(
        left, right, (((1,), (1,)), ((), ())), preferred_element_type=jnp.float32
    )


def swiglu_grads(normed_rows, gate_pre, up_proj, grad_hidden):
    sigmoid_g = jax.nn.sigmoid(gate_pre)
    grad_gate_pre = (
        grad_hidden * up_proj * sigmoid_g * (1.0 + gate_pre * (1.0 - sigmoid_g))
    ).astype(jnp.bfloat16)
    grad_up = (grad_hidden * gate_pre * sigmoid_g).astype(jnp.bfloat16)
    grad_gate_up = jnp.stack(
        [contract_rows(normed_rows, grad_gate_pre), contract_rows(normed_rows, grad_up)]
    )
    return (grad_gate_pre, grad_up, grad_gate_up)


def per_device(
    tokens,
    segment_ids,
    gain_in,
    w_qkv,
    conv_w,
    w_decay,
    a_log,
    dt_bias,
    w_gate_o,
    gain_o,
    w_out,
    gain_mid,
    w_gate_up,
    w_down,
    cotangent,
):
    segments = segment_ids[0]
    residual_in = tokens.astype(jnp.float32)
    normed_f, norm_in_back = jax.vjp(rms_scale, residual_in, gain_in)
    normed_in = normed_f.astype(jnp.bfloat16)
    raw_proj = jnp.dot(normed_in, w_qkv, preferred_element_type=jnp.float32)
    gate_logits = jnp.dot(normed_in, w_decay, preferred_element_type=jnp.float32)
    out_gate = jnp.dot(normed_in, w_gate_o, preferred_element_type=jnp.float32)

    def local_mixer(raw_a, logit_a, gate_a, conv_a, log_a, bias_a, gain_a):
        return mixer(raw_a, logit_a, gate_a, segments, conv_a, log_a, bias_a, gain_a)

    mixed_f, mixer_back = jax.vjp(
        local_mixer, raw_proj, gate_logits, out_gate, conv_w, a_log, dt_bias, gain_o
    )
    mixed = mixed_f.astype(jnp.bfloat16)
    middle = residual_in + jnp.dot(mixed, w_out, preferred_element_type=jnp.float32)
    normed_mf, norm_mid_back = jax.vjp(rms_scale, middle, gain_mid)
    normed_mid = normed_mf.astype(jnp.bfloat16)
    gate_up_rows, down_rows = (
        lax.all_gather(w_gate_up, "row", axis=1, tiled=True),
        lax.all_gather(w_down, "row", axis=1, tiled=True),
    )
    normed_all = lax.all_gather(normed_mid, "col", axis=0, tiled=True)
    gate_pre = jnp.dot(normed_all, gate_up_rows[0], preferred_element_type=jnp.float32)
    up_proj = jnp.dot(normed_all, gate_up_rows[1], preferred_element_type=jnp.float32)
    hidden = (jax.nn.silu(gate_pre) * up_proj).astype(jnp.bfloat16)
    ffn_out = lax.psum_scatter(
        jnp.dot(hidden, down_rows, preferred_element_type=jnp.float32).astype(jnp.bfloat16),
        "col",
        scatter_dimension=0,
        tiled=True,
    ).astype(jnp.float32)
    block_out = (middle + ffn_out).astype(jnp.bfloat16)
    cot_all = lax.all_gather(cotangent, "col", axis=0, tiled=True)
    grad_hidden = contract_cols(cot_all, down_rows)
    grad_gate_pre, grad_up, grad_gu_part = swiglu_grads(normed_all, gate_pre, up_proj, grad_hidden)
    grad_down_part = contract_rows(hidden, cot_all)
    grad_normed_mid = lax.psum_scatter(
        contract_cols(grad_gate_pre, gate_up_rows[0]) + contract_cols(grad_up, gate_up_rows[1]),
        "col",
        scatter_dimension=0,
        tiled=True,
    )
    grad_gate_up, grad_down = (
        lax.psum_scatter(
            grad_gu_part.astype(jnp.bfloat16), "row", scatter_dimension=1, tiled=True
        ).astype(jnp.float32),
        lax.psum_scatter(
            grad_down_part.astype(jnp.bfloat16), "row", scatter_dimension=1, tiled=True
        ).astype(jnp.float32),
    )
    grad_mid_norm, grad_gain_mid = norm_mid_back(grad_normed_mid)
    grad_middle = cotangent.astype(jnp.float32) + grad_mid_norm
    grad_middle_b = grad_middle.astype(jnp.bfloat16)
    grad_out = contract_rows(mixed, grad_middle_b)
    grad_mixed = contract_cols(grad_middle_b, w_out)
    grad_raw, grad_logits, grad_gate_out, grad_conv, grad_a_log, grad_dt_bias, grad_gain_o = (
        mixer_back(grad_mixed)
    )
    grad_raw_b = grad_raw.astype(jnp.bfloat16)
    grad_logits_b = grad_logits.astype(jnp.bfloat16)
    grad_gate_b = grad_gate_out.astype(jnp.bfloat16)
    grad_qkv = contract_rows(normed_in, grad_raw_b)
    grad_decay = contract_rows(normed_in, grad_logits_b)
    grad_gate_o = contract_rows(normed_in, grad_gate_b)
    grad_normed_in = (
        contract_cols(grad_raw_b, w_qkv)
        + contract_cols(grad_logits_b, w_decay)
        + contract_cols(grad_gate_b, w_gate_o)
    )
    grad_in_norm, grad_gain_in = norm_in_back(grad_normed_in)
    grad_tokens = grad_middle + grad_in_norm
    summed = lax.psum(
        (
            grad_gain_in,
            grad_qkv,
            grad_conv,
            grad_decay,
            grad_a_log,
            grad_dt_bias,
            grad_gate_o,
            grad_gain_o,
            grad_out,
            grad_gain_mid,
        ),
        ("row", "col"),
    )
    return (
        block_out,
        grad_tokens,
        summed[0],
        summed[1],
        summed[2],
        summed[3],
        summed[4],
        summed[5],
        summed[6],
        summed[7],
        summed[8],
        summed[9],
        grad_gate_up,
        grad_down,
    )


def solution(mesh):
    in_specs = (
        P(("row", "col"), None),
        P(("row", "col"), None),
        P(),
        P(),
        P(),
        P(),
        P(),
        P(),
        P(),
        P(),
        P(),
        P(),
        P(None, "row", "col"),
        P("col", "row"),
        P(("row", "col"), None),
    )
    out_specs = (
        P(("row", "col"), None),
        P(("row", "col"), None),
        P(),
        P(),
        P(),
        P(),
        P(),
        P(),
        P(),
        P(),
        P(),
        P(),
        P(None, "row", "col"),
        P("col", "row"),
    )
    return jax.shard_map(
        per_device, mesh=mesh, in_specs=in_specs, out_specs=out_specs, check_vma=False
    )
```

```python
import jax
import jax.numpy as jnp
from jax import lax
from jax.sharding import PartitionSpec as P

HEADS = 6
HEAD_K = 128
HEAD_V = 256
CONV = 4
STRETCH = 64
HI = lax.Precision.HIGHEST


EPSILON = 1e-06


def rms_scale(values, gain_vec):
    return (
        values * lax.rsqrt(jnp.mean(values * values, axis=-1, keepdims=True) + EPSILON) * gain_vec
    )


def conv_silu(raw_proj, conv_weight, segments):
    length = raw_proj.shape[0]
    mixed = raw_proj * conv_weight[CONV - 1]
    for offset in range(1, CONV):
        shifted = jnp.concatenate(
            [jnp.zeros((offset, raw_proj.shape[1]), jnp.float32), raw_proj[: length - offset]],
            axis=0,
        )
        seg_shifted = jnp.concatenate(
            [jnp.full((offset,), -1, jnp.int32), segments[: length - offset]], axis=0
        )
        keep_tap = (seg_shifted == segments).astype(jnp.float32)[:, None]
        mixed = mixed + shifted * keep_tap * conv_weight[CONV - 1 - offset]
    return jax.nn.silu(mixed)


def head_blocks(array, stretch_count):
    shaped = array.reshape((stretch_count, STRETCH) + array.shape[1:])
    return jnp.swapaxes(shaped, 1, 2)


LEAF = 8


def _mm(a, b):
    return jnp.einsum("...ij,...jk->...ik", a, b, precision=HI)


def _unit_lower_inverse_fwd_impl(strict_part):
    n = strict_part.shape[-1]
    lead = strict_part.shape[:-2]
    nb = n // LEAF
    eye = jnp.eye(LEAF, dtype=strict_part.dtype)
    diag = jnp.stack(
        [strict_part[..., i * LEAF:(i + 1) * LEAF, i * LEAF:(i + 1) * LEAF] for i in range(nb)], axis=-3
    )
    sq = _mm(diag, diag)
    blocks = _mm(_mm(eye - diag, eye + sq), eye + _mm(sq, sq))
    size = LEAF
    while size < n:
        count = n // (2 * size)
        upper_inv = blocks[..., 0::2, :, :]
        lower_inv = blocks[..., 1::2, :, :]
        cross = jnp.stack(
            [strict_part[..., (2 * p + 1) * size:(2 * p + 2) * size, 2 * p * size:(2 * p + 1) * size] for p in range(count)],
            axis=-3,
        )
        corner = -_mm(lower_inv, _mm(cross, upper_inv))
        zeros = jnp.zeros_like(corner)
        top = jnp.concatenate([upper_inv, zeros], axis=-1)
        bottom = jnp.concatenate([corner, lower_inv], axis=-1)
        blocks = jnp.concatenate([top, bottom], axis=-2)
        size *= 2
    return blocks[..., 0, :, :]


@jax.custom_vjp
def unit_lower_inverse(strict_part):
    return _unit_lower_inverse_fwd_impl(strict_part)


def _uli_fwd(strict_part):
    inv = _unit_lower_inverse_fwd_impl(strict_part)
    return inv, inv


def _uli_bwd(inv, grad):
    n = inv.shape[-1]
    below = jnp.arange(n)[:, None] > jnp.arange(n)[None, :]
    inv_t = jnp.swapaxes(inv, -1, -2)
    return (jnp.where(below, -_mm(inv_t, _mm(grad, inv_t)), 0.0),)


unit_lower_inverse.defvjp(_uli_fwd, _uli_bwd)


def delta_rule(queries, keys_unit, values_part, log_decay, write_rate, segments):
    length = queries.shape[0]
    nc = length // STRETCH
    q = head_blocks(queries, nc)
    k = head_blocks(keys_unit, nc)
    v = head_blocks(values_part, nc)
    g = head_blocks(log_decay, nc)
    beta = head_blocks(write_rate, nc)
    seg = segments.reshape(nc, STRETCH)
    seg_prev = jnp.concatenate([jnp.full((1,), -1, jnp.int32), seg[:-1, -1]], axis=0)
    row = jnp.arange(STRETCH)[:, None]
    col = jnp.arange(STRETCH)[None, :]
    cum = jnp.cumsum(g, axis=-1)
    live = ((seg[:, :, None] == seg[:, None, :]) & (row >= col))[:, None]
    gap = cum[..., :, None] - cum[..., None, :]
    decay_mat = jnp.where(live, jnp.exp(jnp.where(live, gap, 0.0)), 0.0)
    carry = jnp.exp(cum) * (seg == seg_prev[:, None]).astype(jnp.float32)[:, None, :]
    gram = jnp.einsum("nhck,nhsk->nhcs", k, k, precision=HI)
    strict = jnp.where((row > col)[None, None], decay_mat, 0.0)
    inverse = unit_lower_inverse(beta[..., None] * strict * gram)
    rhs = jnp.concatenate([beta[..., None] * v, (beta * carry)[..., None] * k], axis=-1)
    sol = jnp.einsum("nhcs,nhsv->nhcv", inverse, rhs, precision=HI)
    u, w = sol[..., :HEAD_V], sol[..., HEAD_V:]
    kw = k * decay_mat[..., -1, :, None]
    m = jnp.einsum("nhck,nhcj->nhkj", kw, w, precision=HI)
    nn = jnp.einsum("nhck,nhcv->nhkv", kw, u, precision=HI)
    a_last = carry[..., -1]
    states = [jnp.zeros((HEADS, HEAD_K, HEAD_V), jnp.float32)]
    s = nn[0]
    states.append(s)
    for c in range(1, nc - 1):
        s = a_last[c][:, None, None] * s - jnp.einsum("hkj,hjv->hkv", m[c], s, precision=HI) + nn[c]
        states.append(s)
    st = jnp.stack(states)
    p = u - jnp.einsum("nhck,nhkv->nhcv", w, st, precision=HI)
    scores = jnp.einsum("nhck,nhsk->nhcs", q, k, precision=HI) * decay_mat
    out = carry[..., None] * jnp.einsum("nhck,nhkv->nhcv", q, st, precision=HI)
    out = out + jnp.einsum("nhcs,nhsv->nhcv", scores, p, precision=HI)
    return jnp.swapaxes(out, 1, 2).reshape(length, HEADS, HEAD_V)


def mixer(raw_proj, gate_logits, out_gate, segments, conv_weight, a_log, dt_bias, gain_o):
    length = raw_proj.shape[0]
    key_dim = HEADS * HEAD_K
    conv = conv_silu(raw_proj, conv_weight, segments)
    queries = conv[:, :key_dim].reshape(length, HEADS, HEAD_K)
    keys_raw = conv[:, key_dim : 2 * key_dim].reshape(length, HEADS, HEAD_K)
    values_part = conv[:, 2 * key_dim :].reshape(length, HEADS, HEAD_V)
    queries = (
        queries
        * lax.rsqrt(jnp.sum(queries * queries, axis=-1, keepdims=True) + EPSILON)
        * HEAD_K ** (-0.5)
    )
    keys_unit = keys_raw * lax.rsqrt(jnp.sum(keys_raw * keys_raw, axis=-1, keepdims=True) + EPSILON)
    log_decay = -jnp.exp(a_log) * jax.nn.softplus(gate_logits[:, :HEADS] + dt_bias)
    write_rate = jax.nn.sigmoid(gate_logits[:, HEADS:])
    delta_out = delta_rule(queries, keys_unit, values_part, log_decay, write_rate, segments)
    gate_vals = jax.nn.silu(out_gate).reshape(length, HEADS, HEAD_V)
    normed = (
        delta_out
        * lax.rsqrt(jnp.mean(delta_out * delta_out, axis=-1, keepdims=True) + EPSILON)
        * gain_o
        * gate_vals
    )
    return normed.reshape(length, HEADS * HEAD_V)


def contract_rows(left, right):
    return lax.dot_general(
        left, right, (((0,), (0,)), ((), ())), preferred_element_type=jnp.float32
    )


def contract_cols(left, right):
    return lax.dot_general(
        left, right, (((1,), (1,)), ((), ())), preferred_element_type=jnp.float32
    )


def swiglu_grads(normed_rows, gate_pre, up_proj, grad_hidden):
    sigmoid_g = jax.nn.sigmoid(gate_pre)
    grad_gate_pre = (
        grad_hidden * up_proj * sigmoid_g * (1.0 + gate_pre * (1.0 - sigmoid_g))
    ).astype(jnp.bfloat16)
    grad_up = (grad_hidden * gate_pre * sigmoid_g).astype(jnp.bfloat16)
    grad_gate_up = jnp.stack(
        [contract_rows(normed_rows, grad_gate_pre), contract_rows(normed_rows, grad_up)]
    )
    return (grad_gate_pre, grad_up, grad_gate_up)


def per_device(
    tokens,
    segment_ids,
    gain_in,
    w_qkv,
    conv_w,
    w_decay,
    a_log,
    dt_bias,
    w_gate_o,
    gain_o,
    w_out,
    gain_mid,
    w_gate_up,
    w_down,
    cotangent,
):
    segments = segment_ids[0]
    residual_in = tokens.astype(jnp.float32)
    normed_f, norm_in_back = jax.vjp(rms_scale, residual_in, gain_in)
    normed_in = normed_f.astype(jnp.bfloat16)
    raw_proj = jnp.dot(normed_in, w_qkv, preferred_element_type=jnp.float32)
    gate_logits = jnp.dot(normed_in, w_decay, preferred_element_type=jnp.float32)
    out_gate = jnp.dot(normed_in, w_gate_o, preferred_element_type=jnp.float32)

    def local_mixer(raw_a, logit_a, gate_a, conv_a, log_a, bias_a, gain_a):
        return mixer(raw_a, logit_a, gate_a, segments, conv_a, log_a, bias_a, gain_a)

    mixed_f, mixer_back = jax.vjp(
        local_mixer, raw_proj, gate_logits, out_gate, conv_w, a_log, dt_bias, gain_o
    )
    mixed = mixed_f.astype(jnp.bfloat16)
    gate_up_rows, down_rows = (
        lax.all_gather(w_gate_up, "row", axis=1, tiled=True),
        lax.all_gather(w_down, "row", axis=1, tiled=True),
    )
    cot_all = lax.all_gather(cotangent, "col", axis=0, tiled=True)
    mixed, gate_up_rows, down_rows, cot_all = lax.optimization_barrier(
        (mixed, gate_up_rows, down_rows, cot_all)
    )
    middle = residual_in + jnp.dot(mixed, w_out, preferred_element_type=jnp.float32)
    normed_mf, norm_mid_back = jax.vjp(rms_scale, middle, gain_mid)
    normed_mid = normed_mf.astype(jnp.bfloat16)
    normed_all = lax.all_gather(normed_mid, "col", axis=0, tiled=True)
    gate_pre = jnp.dot(normed_all, gate_up_rows[0], preferred_element_type=jnp.float32)
    up_proj = jnp.dot(normed_all, gate_up_rows[1], preferred_element_type=jnp.float32)
    hidden = (jax.nn.silu(gate_pre) * up_proj).astype(jnp.bfloat16)
    ffn_part = jnp.dot(hidden, down_rows, preferred_element_type=jnp.float32).astype(jnp.bfloat16)
    grad_hidden = contract_cols(cot_all, down_rows)
    grad_gate_pre, grad_up, grad_gu_part = swiglu_grads(normed_all, gate_pre, up_proj, grad_hidden)
    grad_down_part = contract_rows(hidden, cot_all)
    grad_normed_mid = lax.psum_scatter(
        contract_cols(grad_gate_pre, gate_up_rows[0]) + contract_cols(grad_up, gate_up_rows[1]),
        "col",
        scatter_dimension=0,
        tiled=True,
    )
    grad_normed_mid, ffn_part, grad_gu_part, grad_down_part = lax.optimization_barrier(
        (grad_normed_mid, ffn_part, grad_gu_part, grad_down_part)
    )
    ffn_out = lax.psum_scatter(ffn_part, "col", scatter_dimension=0, tiled=True)
    grad_gate_up, grad_down = (
        lax.psum_scatter(
            grad_gu_part.astype(jnp.bfloat16), "row", scatter_dimension=1, tiled=True
        ).astype(jnp.float32),
        lax.psum_scatter(
            grad_down_part.astype(jnp.bfloat16), "row", scatter_dimension=1, tiled=True
        ).astype(jnp.float32),
    )
    grad_mid_norm, grad_gain_mid = norm_mid_back(grad_normed_mid)
    grad_middle = cotangent.astype(jnp.float32) + grad_mid_norm
    grad_middle_b = grad_middle.astype(jnp.bfloat16)
    grad_out = contract_rows(mixed, grad_middle_b)
    grad_mixed = contract_cols(grad_middle_b, w_out)
    grad_raw, grad_logits, grad_gate_out, grad_conv, grad_a_log, grad_dt_bias, grad_gain_o = (
        mixer_back(grad_mixed)
    )
    grad_raw_b = grad_raw.astype(jnp.bfloat16)
    grad_logits_b = grad_logits.astype(jnp.bfloat16)
    grad_gate_b = grad_gate_out.astype(jnp.bfloat16)
    ffn_out, grad_raw_b = lax.optimization_barrier((ffn_out, grad_raw_b))
    block_out = (middle + ffn_out.astype(jnp.float32)).astype(jnp.bfloat16)
    grad_qkv = contract_rows(normed_in, grad_raw_b)
    grad_decay = contract_rows(normed_in, grad_logits_b)
    grad_gate_o = contract_rows(normed_in, grad_gate_b)
    early = summed_bf16((grad_out, grad_gate_o))
    grad_normed_in = (
        contract_cols(grad_raw_b, w_qkv)
        + contract_cols(grad_logits_b, w_decay)
        + contract_cols(grad_gate_b, w_gate_o)
    )
    grad_in_norm, grad_gain_in = norm_in_back(grad_normed_in)
    grad_tokens = grad_middle + grad_in_norm
    late = summed_bf16((grad_qkv,), after=early[0])
    small = summed_f32(
        (grad_gain_in, grad_conv, grad_decay, grad_a_log, grad_dt_bias, grad_gain_o, grad_gain_mid)
    )
    return (
        block_out,
        grad_tokens,
        small[0],
        late[0],
        small[1],
        small[2],
        small[3],
        small[4],
        early[1],
        small[5],
        early[0],
        small[6],
        grad_gate_up,
        grad_down,
    )


def split_flat(total, parts):
    out, at = [], 0
    for p in parts:
        out.append(total[at : at + p.size].reshape(p.shape).astype(jnp.float32))
        at += p.size
    return out


def summed_f32(parts):
    flat = jnp.concatenate([p.reshape(-1) for p in parts])
    for axis in ("col", "row"):
        n = lax.axis_size(axis)
        if n & (n - 1):
            flat = lax.psum(flat, axis)
            continue
        step = 1
        while step < n:
            flat = flat + lax.ppermute(flat, axis, [(i, i ^ step) for i in range(n)])
            step *= 2
    return split_flat(flat, parts)


def summed_bf16(parts, after=None):
    flat = jnp.concatenate([p.astype(jnp.bfloat16).reshape(-1) for p in parts])
    if after is not None:
        flat, _ = lax.optimization_barrier((flat, after))
    return split_flat(lax.psum(flat, ("row", "col")), parts)


def solution(mesh):
    in_specs = (
        P(("row", "col"), None),
        P(("row", "col"), None),
        P(),
        P(),
        P(),
        P(),
        P(),
        P(),
        P(),
        P(),
        P(),
        P(),
        P(None, "row", "col"),
        P("col", "row"),
        P(("row", "col"), None),
    )
    out_specs = (
        P(("row", "col"), None),
        P(("row", "col"), None),
        P(),
        P(),
        P(),
        P(),
        P(),
        P(),
        P(),
        P(),
        P(),
        P(),
        P(None, "row", "col"),
        P("col", "row"),
    )
    return jax.shard_map(
        per_device, mesh=mesh, in_specs=in_specs, out_specs=out_specs, check_vma=False
    )
```

```python
import jax
import jax.numpy as jnp
from jax import lax
from jax.sharding import PartitionSpec as P

HEADS = 6
HEAD_K = 128
HEAD_V = 256
CONV = 4
STRETCH = 64
HI = lax.Precision.HIGHEST


EPSILON = 1e-06


def rms_scale(values, gain_vec):
    return (
        values * lax.rsqrt(jnp.mean(values * values, axis=-1, keepdims=True) + EPSILON) * gain_vec
    )


def conv_silu(raw_proj, conv_weight, segments):
    length = raw_proj.shape[0]
    mixed = raw_proj * conv_weight[CONV - 1]
    for offset in range(1, CONV):
        shifted = jnp.concatenate(
            [jnp.zeros((offset, raw_proj.shape[1]), jnp.float32), raw_proj[: length - offset]],
            axis=0,
        )
        seg_shifted = jnp.concatenate(
            [jnp.full((offset,), -1, jnp.int32), segments[: length - offset]], axis=0
        )
        keep_tap = (seg_shifted == segments).astype(jnp.float32)[:, None]
        mixed = mixed + shifted * keep_tap * conv_weight[CONV - 1 - offset]
    return jax.nn.silu(mixed)


def head_blocks(array, stretch_count):
    shaped = array.reshape((stretch_count, STRETCH) + array.shape[1:])
    return jnp.swapaxes(shaped, 1, 2)


LEAF = 8


def _mm(a, b):
    return jnp.einsum("...ij,...jk->...ik", a, b, precision=HI)


def _unit_lower_inverse_fwd_impl(strict_part):
    n = strict_part.shape[-1]
    nb = n // LEAF
    eye = jnp.eye(LEAF, dtype=strict_part.dtype)
    diag = jnp.stack(
        [strict_part[..., i * LEAF:(i + 1) * LEAF, i * LEAF:(i + 1) * LEAF] for i in range(nb)], axis=-3
    )
    sq = _mm(diag, diag)
    blocks = _mm(_mm(eye - diag, eye + sq), eye + _mm(sq, sq))
    size = LEAF
    while size < n:
        count = n // (2 * size)
        upper_inv = blocks[..., 0::2, :, :]
        lower_inv = blocks[..., 1::2, :, :]
        cross = jnp.stack(
            [strict_part[..., (2 * p + 1) * size:(2 * p + 2) * size, 2 * p * size:(2 * p + 1) * size] for p in range(count)],
            axis=-3,
        )
        corner = -_mm(lower_inv, _mm(cross, upper_inv))
        zeros = jnp.zeros_like(corner)
        top = jnp.concatenate([upper_inv, zeros], axis=-1)
        bottom = jnp.concatenate([corner, lower_inv], axis=-1)
        blocks = jnp.concatenate([top, bottom], axis=-2)
        size *= 2
    return blocks[..., 0, :, :]


@jax.custom_vjp
def unit_lower_inverse(strict_part):
    return _unit_lower_inverse_fwd_impl(strict_part)


def _uli_fwd(strict_part):
    inv = _unit_lower_inverse_fwd_impl(strict_part)
    return inv, inv


def _uli_bwd(inv, grad):
    n = inv.shape[-1]
    below = jnp.arange(n)[:, None] > jnp.arange(n)[None, :]
    inv_t = jnp.swapaxes(inv, -1, -2)
    return (jnp.where(below, -_mm(inv_t, _mm(grad, inv_t)), 0.0),)


unit_lower_inverse.defvjp(_uli_fwd, _uli_bwd)


def delta_rule(queries, keys_unit, values_part, log_decay, write_rate, segments):
    length = queries.shape[0]
    nc = length // STRETCH
    q = head_blocks(queries, nc)
    k = head_blocks(keys_unit, nc)
    v = head_blocks(values_part, nc)
    g = head_blocks(log_decay, nc)
    beta = head_blocks(write_rate, nc)
    seg = segments.reshape(nc, STRETCH)
    seg_prev = jnp.concatenate([jnp.full((1,), -1, jnp.int32), seg[:-1, -1]], axis=0)
    row = jnp.arange(STRETCH)[:, None]
    col = jnp.arange(STRETCH)[None, :]
    cum = jnp.cumsum(g, axis=-1)
    live = ((seg[:, :, None] == seg[:, None, :]) & (row >= col))[:, None]
    gap = cum[..., :, None] - cum[..., None, :]
    decay_mat = jnp.where(live, jnp.exp(jnp.where(live, gap, 0.0)), 0.0)
    carry = jnp.exp(cum) * (seg == seg_prev[:, None]).astype(jnp.float32)[:, None, :]
    gram = jnp.einsum("nhck,nhsk->nhcs", k, k, precision=HI)
    strict = jnp.where((row > col)[None, None], decay_mat, 0.0)
    inverse = unit_lower_inverse(beta[..., None] * strict * gram)
    rhs = jnp.concatenate([beta[..., None] * v, (beta * carry)[..., None] * k], axis=-1)
    sol = jnp.einsum("nhcs,nhsv->nhcv", inverse, rhs, precision=HI)
    u, w = sol[..., :HEAD_V], sol[..., HEAD_V:]
    kw = k * decay_mat[..., -1, :, None]
    m = jnp.einsum("nhck,nhcj->nhkj", kw, w, precision=HI)
    nn = jnp.einsum("nhck,nhcv->nhkv", kw, u, precision=HI)
    a_last = carry[..., -1]
    states = [jnp.zeros((HEADS, HEAD_K, HEAD_V), jnp.float32)]
    s = nn[0]
    states.append(s)
    for c in range(1, nc - 1):
        s = a_last[c][:, None, None] * s - jnp.einsum("hkj,hjv->hkv", m[c], s, precision=HI) + nn[c]
        states.append(s)
    st = jnp.stack(states)
    p = u - jnp.einsum("nhck,nhkv->nhcv", w, st, precision=HI)
    scores = jnp.einsum("nhck,nhsk->nhcs", q, k, precision=HI) * decay_mat
    out = carry[..., None] * jnp.einsum("nhck,nhkv->nhcv", q, st, precision=HI)
    out = out + jnp.einsum("nhcs,nhsv->nhcv", scores, p, precision=HI)
    return jnp.swapaxes(out, 1, 2).reshape(length, HEADS, HEAD_V)


def mixer(raw_proj, gate_logits, out_gate, segments, conv_weight, a_log, dt_bias, gain_o):
    length = raw_proj.shape[0]
    key_dim = HEADS * HEAD_K
    conv = conv_silu(raw_proj, conv_weight, segments)
    queries = conv[:, :key_dim].reshape(length, HEADS, HEAD_K)
    keys_raw = conv[:, key_dim : 2 * key_dim].reshape(length, HEADS, HEAD_K)
    values_part = conv[:, 2 * key_dim :].reshape(length, HEADS, HEAD_V)
    queries = (
        queries
        * lax.rsqrt(jnp.sum(queries * queries, axis=-1, keepdims=True) + EPSILON)
        * HEAD_K ** (-0.5)
    )
    keys_unit = keys_raw * lax.rsqrt(jnp.sum(keys_raw * keys_raw, axis=-1, keepdims=True) + EPSILON)
    log_decay = -jnp.exp(a_log) * jax.nn.softplus(gate_logits[:, :HEADS] + dt_bias)
    write_rate = jax.nn.sigmoid(gate_logits[:, HEADS:])
    delta_out = delta_rule(queries, keys_unit, values_part, log_decay, write_rate, segments)
    gate_vals = jax.nn.silu(out_gate).reshape(length, HEADS, HEAD_V)
    normed = (
        delta_out
        * lax.rsqrt(jnp.mean(delta_out * delta_out, axis=-1, keepdims=True) + EPSILON)
        * gain_o
        * gate_vals
    )
    return normed.reshape(length, HEADS * HEAD_V)


def contract_rows(left, right):
    return lax.dot_general(
        left, right, (((0,), (0,)), ((), ())), preferred_element_type=jnp.float32
    )


def contract_cols(left, right):
    return lax.dot_general(
        left, right, (((1,), (1,)), ((), ())), preferred_element_type=jnp.float32
    )


def swiglu_grads(normed_rows, gate_pre, up_proj, grad_hidden):
    sigmoid_g = jax.nn.sigmoid(gate_pre)
    grad_gate_pre = (
        grad_hidden * up_proj * sigmoid_g * (1.0 + gate_pre * (1.0 - sigmoid_g))
    ).astype(jnp.bfloat16)
    grad_up = (grad_hidden * gate_pre * sigmoid_g).astype(jnp.bfloat16)
    grad_gate_up = jnp.stack(
        [contract_rows(normed_rows, grad_gate_pre), contract_rows(normed_rows, grad_up)]
    )
    return (grad_gate_pre, grad_up, grad_gate_up)


def per_device_body(
    tokens,
    segment_ids,
    gain_in,
    w_qkv,
    conv_w,
    w_decay,
    a_log,
    dt_bias,
    w_gate_o,
    gain_o,
    w_out,
    gain_mid,
    w_gate_up,
    w_down,
    cotangent,
):
    segments = segment_ids[0]
    residual_in = tokens.astype(jnp.float32)
    normed_f, norm_in_back = jax.vjp(rms_scale, residual_in, gain_in)
    normed_in = normed_f.astype(jnp.bfloat16)
    raw_proj = jnp.dot(normed_in, w_qkv, preferred_element_type=jnp.float32)
    gate_logits = jnp.dot(normed_in, w_decay, preferred_element_type=jnp.float32)
    out_gate = jnp.dot(normed_in, w_gate_o, preferred_element_type=jnp.float32)

    def local_mixer(raw_a, logit_a, gate_a, conv_a, log_a, bias_a, gain_a):
        return mixer(raw_a, logit_a, gate_a, segments, conv_a, log_a, bias_a, gain_a)

    mixed_f, mixer_back = jax.vjp(
        local_mixer, raw_proj, gate_logits, out_gate, conv_w, a_log, dt_bias, gain_o
    )
    mixed = mixed_f.astype(jnp.bfloat16)
    gate_up_rows, down_rows = (
        lax.all_gather(w_gate_up, "row", axis=1, tiled=True),
        lax.all_gather(w_down, "row", axis=1, tiled=True),
    )
    cot_all = lax.all_gather(cotangent, "col", axis=0, tiled=True)
    mixed, gate_up_rows, down_rows, cot_all = lax.optimization_barrier(
        (mixed, gate_up_rows, down_rows, cot_all)
    )
    middle = residual_in + jnp.dot(mixed, w_out, preferred_element_type=jnp.float32)
    middle_out = lax.optimization_barrier(middle)
    normed_mf, norm_mid_back = jax.vjp(rms_scale, middle, gain_mid)
    normed_mid = normed_mf.astype(jnp.bfloat16)
    normed_all = lax.all_gather(normed_mid, "col", axis=0, tiled=True)
    gate_pre = jnp.dot(normed_all, gate_up_rows[0], preferred_element_type=jnp.float32)
    up_proj = jnp.dot(normed_all, gate_up_rows[1], preferred_element_type=jnp.float32)
    hidden = (jax.nn.silu(gate_pre) * up_proj).astype(jnp.bfloat16)
    ffn_part = jnp.dot(hidden, down_rows, preferred_element_type=jnp.float32).astype(jnp.bfloat16)
    grad_hidden = contract_cols(cot_all, down_rows)
    grad_gate_pre, grad_up, grad_gu_part = swiglu_grads(normed_all, gate_pre, up_proj, grad_hidden)
    grad_down_part = contract_rows(hidden, cot_all)
    grad_nm_part = (
        contract_cols(grad_gate_pre, gate_up_rows[0]) + contract_cols(grad_up, gate_up_rows[1])
    ).astype(jnp.bfloat16)
    grad_normed_mid = lax.psum_scatter(grad_nm_part, "col", scatter_dimension=0, tiled=True)
    grad_normed_mid = grad_normed_mid.astype(jnp.float32)
    ffn_out = lax.psum_scatter(ffn_part, "col", scatter_dimension=0, tiled=True)
    grad_gate_up, grad_down = (
        lax.psum_scatter(
            grad_gu_part.astype(jnp.bfloat16), "row", scatter_dimension=1, tiled=True
        ).astype(jnp.float32),
        lax.psum_scatter(
            grad_down_part.astype(jnp.bfloat16), "row", scatter_dimension=1, tiled=True
        ).astype(jnp.float32),
    )
    grad_mid_norm, grad_gain_mid = norm_mid_back(grad_normed_mid)
    grad_middle = cotangent.astype(jnp.float32) + grad_mid_norm
    grad_middle_b = grad_middle.astype(jnp.bfloat16)
    grad_out = contract_rows(mixed, grad_middle_b)
    grad_mixed = contract_cols(grad_middle_b, w_out)
    grad_raw, grad_logits, grad_gate_out, grad_conv, grad_a_log, grad_dt_bias, grad_gain_o = (
        mixer_back(grad_mixed)
    )
    grad_raw_b = grad_raw.astype(jnp.bfloat16)
    grad_logits_b = grad_logits.astype(jnp.bfloat16)
    grad_gate_b = grad_gate_out.astype(jnp.bfloat16)
    grad_qkv = contract_rows(normed_in, grad_raw_b)
    grad_decay = contract_rows(normed_in, grad_logits_b)
    grad_gate_o = contract_rows(normed_in, grad_gate_b)
    early = summed_bf16((grad_out, grad_gate_o))
    block_out = (middle_out + ffn_out.astype(jnp.float32)).astype(jnp.bfloat16)
    grad_normed_in = (
        contract_cols(grad_raw_b, w_qkv)
        + contract_cols(grad_logits_b, w_decay)
        + contract_cols(grad_gate_b, w_gate_o)
    )
    grad_in_norm, grad_gain_in = norm_in_back(grad_normed_in)
    grad_tokens = grad_middle + grad_in_norm
    late = summed_bf16((grad_qkv,), after=early[0])
    small = summed_f32(
        (grad_gain_in, grad_conv, grad_decay, grad_a_log, grad_dt_bias, grad_gain_o, grad_gain_mid)
    )
    return (
        block_out,
        grad_tokens,
        small[0],
        late[0],
        small[1],
        small[2],
        small[3],
        small[4],
        early[1],
        small[5],
        early[0],
        small[6],
        grad_gate_up,
        grad_down,
    )


def split_flat(total, parts):
    out, at = [], 0
    for p in parts:
        out.append(total[at : at + p.size].reshape(p.shape).astype(jnp.float32))
        at += p.size
    return out


def summed_f32(parts):
    flat = jnp.concatenate([p.reshape(-1) for p in parts])
    for axis in ("col", "row"):
        n = lax.axis_size(axis)
        if n & (n - 1):
            flat = lax.psum(flat, axis)
            continue
        step = 1
        while step < n:
            flat = flat + lax.ppermute(flat, axis, [(i, i ^ step) for i in range(n)])
            step *= 2
    return split_flat(flat, parts)


def summed_bf16(parts, after=None):
    flat = jnp.concatenate([p.astype(jnp.bfloat16).reshape(-1) for p in parts])
    if after is not None:
        flat, _ = lax.optimization_barrier((flat, after))
    return split_flat(lax.psum(flat, ("row", "col")), parts)


def solution(mesh):
    in_specs = (
        P(("row", "col"), None),
        P(("row", "col"), None),
        P(),
        P(),
        P(),
        P(),
        P(),
        P(),
        P(),
        P(),
        P(),
        P(),
        P(None, "row", "col"),
        P("col", "row"),
        P(("row", "col"), None),
    )
    out_specs = (
        P(("row", "col"), None),
        P(("row", "col"), None),
        P(),
        P(),
        P(),
        P(),
        P(),
        P(),
        P(),
        P(),
        P(),
        P(),
        P(None, "row", "col"),
        P("col", "row"),
    )
    return jax.shard_map(
        per_device_body, mesh=mesh, in_specs=in_specs, out_specs=out_specs, check_vma=False
    )
```

```python
import jax
import jax.numpy as jnp
from jax import lax
from jax.sharding import PartitionSpec as P

HEADS = 6
HEAD_K = 128
HEAD_V = 256
CONV = 4
STRETCH = 64
HI = lax.Precision.HIGHEST


EPSILON = 1e-06


def rms_scale(values, gain_vec):
    return (
        values * lax.rsqrt(jnp.mean(values * values, axis=-1, keepdims=True) + EPSILON) * gain_vec
    )


def conv_silu(raw_proj, conv_weight, segments):
    length = raw_proj.shape[0]
    mixed = raw_proj * conv_weight[CONV - 1]
    for offset in range(1, CONV):
        shifted = jnp.concatenate(
            [jnp.zeros((offset, raw_proj.shape[1]), jnp.float32), raw_proj[: length - offset]],
            axis=0,
        )
        seg_shifted = jnp.concatenate(
            [jnp.full((offset,), -1, jnp.int32), segments[: length - offset]], axis=0
        )
        keep_tap = (seg_shifted == segments).astype(jnp.float32)[:, None]
        mixed = mixed + shifted * keep_tap * conv_weight[CONV - 1 - offset]
    return jax.nn.silu(mixed)


def head_blocks(array, stretch_count):
    shaped = array.reshape((stretch_count, STRETCH) + array.shape[1:])
    return jnp.swapaxes(shaped, 1, 2)


LEAF = 8


def _mm(a, b):
    return jnp.einsum("...ij,...jk->...ik", a, b, precision=HI)


def _unit_lower_inverse_fwd_impl(strict_part):
    n = strict_part.shape[-1]
    nb = n // LEAF
    eye = jnp.eye(LEAF, dtype=strict_part.dtype)
    diag = jnp.stack(
        [strict_part[..., i * LEAF:(i + 1) * LEAF, i * LEAF:(i + 1) * LEAF] for i in range(nb)], axis=-3
    )
    sq = _mm(diag, diag)
    blocks = _mm(_mm(eye - diag, eye + sq), eye + _mm(sq, sq))
    size = LEAF
    while size < n:
        count = n // (2 * size)
        upper_inv = blocks[..., 0::2, :, :]
        lower_inv = blocks[..., 1::2, :, :]
        cross = jnp.stack(
            [strict_part[..., (2 * p + 1) * size:(2 * p + 2) * size, 2 * p * size:(2 * p + 1) * size] for p in range(count)],
            axis=-3,
        )
        corner = -_mm(lower_inv, _mm(cross, upper_inv))
        zeros = jnp.zeros_like(corner)
        top = jnp.concatenate([upper_inv, zeros], axis=-1)
        bottom = jnp.concatenate([corner, lower_inv], axis=-1)
        blocks = jnp.concatenate([top, bottom], axis=-2)
        size *= 2
    return blocks[..., 0, :, :]


@jax.custom_vjp
def unit_lower_inverse(strict_part):
    return _unit_lower_inverse_fwd_impl(strict_part)


def _uli_fwd(strict_part):
    inv = _unit_lower_inverse_fwd_impl(strict_part)
    return inv, inv


def _uli_bwd(inv, grad):
    n = inv.shape[-1]
    below = jnp.arange(n)[:, None] > jnp.arange(n)[None, :]
    inv_t = jnp.swapaxes(inv, -1, -2)
    return (jnp.where(below, -_mm(inv_t, _mm(grad, inv_t)), 0.0),)


unit_lower_inverse.defvjp(_uli_fwd, _uli_bwd)


def delta_rule(queries, keys_unit, values_part, log_decay, write_rate, segments):
    length = queries.shape[0]
    nc = length // STRETCH
    q = head_blocks(queries, nc)
    k = head_blocks(keys_unit, nc)
    v = head_blocks(values_part, nc)
    g = head_blocks(log_decay, nc)
    beta = head_blocks(write_rate, nc)
    seg = segments.reshape(nc, STRETCH)
    seg_prev = jnp.concatenate([jnp.full((1,), -1, jnp.int32), seg[:-1, -1]], axis=0)
    row = jnp.arange(STRETCH)[:, None]
    col = jnp.arange(STRETCH)[None, :]
    cum = jnp.cumsum(g, axis=-1)
    live = ((seg[:, :, None] == seg[:, None, :]) & (row >= col))[:, None]
    gap = cum[..., :, None] - cum[..., None, :]
    decay_mat = jnp.where(live, jnp.exp(jnp.where(live, gap, 0.0)), 0.0)
    carry = jnp.exp(cum) * (seg == seg_prev[:, None]).astype(jnp.float32)[:, None, :]
    gram = jnp.einsum("nhck,nhsk->nhcs", k, k, precision=HI)
    strict = jnp.where((row > col)[None, None], decay_mat, 0.0)
    inverse = unit_lower_inverse(beta[..., None] * strict * gram)
    rhs = jnp.concatenate([beta[..., None] * v, (beta * carry)[..., None] * k], axis=-1)
    sol = jnp.einsum("nhcs,nhsv->nhcv", inverse, rhs, precision=HI)
    u, w = sol[..., :HEAD_V], sol[..., HEAD_V:]
    kw = k * decay_mat[..., -1, :, None]
    m = jnp.einsum("nhck,nhcj->nhkj", kw, w, precision=HI)
    nn = jnp.einsum("nhck,nhcv->nhkv", kw, u, precision=HI)
    a_last = carry[..., -1]
    states = [jnp.zeros((HEADS, HEAD_K, HEAD_V), jnp.float32)]
    s = nn[0]
    states.append(s)
    for c in range(1, nc - 1):
        s = a_last[c][:, None, None] * s - jnp.einsum("hkj,hjv->hkv", m[c], s, precision=HI) + nn[c]
        states.append(s)
    st = jnp.stack(states)
    p = u - jnp.einsum("nhck,nhkv->nhcv", w, st, precision=HI)
    scores = jnp.einsum("nhck,nhsk->nhcs", q, k, precision=HI) * decay_mat
    out = carry[..., None] * jnp.einsum("nhck,nhkv->nhcv", q, st, precision=HI)
    out = out + jnp.einsum("nhcs,nhsv->nhcv", scores, p, precision=HI)
    return jnp.swapaxes(out, 1, 2).reshape(length, HEADS, HEAD_V)


def mixer(raw_proj, gate_logits, out_gate, segments, conv_weight, a_log, dt_bias, gain_o):
    length = raw_proj.shape[0]
    key_dim = HEADS * HEAD_K
    conv = conv_silu(raw_proj, conv_weight, segments)
    queries = conv[:, :key_dim].reshape(length, HEADS, HEAD_K)
    keys_raw = conv[:, key_dim : 2 * key_dim].reshape(length, HEADS, HEAD_K)
    values_part = conv[:, 2 * key_dim :].reshape(length, HEADS, HEAD_V)
    queries = (
        queries
        * lax.rsqrt(jnp.sum(queries * queries, axis=-1, keepdims=True) + EPSILON)
        * HEAD_K ** (-0.5)
    )
    keys_unit = keys_raw * lax.rsqrt(jnp.sum(keys_raw * keys_raw, axis=-1, keepdims=True) + EPSILON)
    log_decay = -jnp.exp(a_log) * jax.nn.softplus(gate_logits[:, :HEADS] + dt_bias)
    write_rate = jax.nn.sigmoid(gate_logits[:, HEADS:])
    delta_out = delta_rule(queries, keys_unit, values_part, log_decay, write_rate, segments)
    gate_vals = jax.nn.silu(out_gate).reshape(length, HEADS, HEAD_V)
    normed = (
        delta_out
        * lax.rsqrt(jnp.mean(delta_out * delta_out, axis=-1, keepdims=True) + EPSILON)
        * gain_o
        * gate_vals
    )
    return normed.reshape(length, HEADS * HEAD_V)


def contract_rows(left, right):
    return lax.dot_general(
        left, right, (((0,), (0,)), ((), ())), preferred_element_type=jnp.float32
    )


def contract_cols(left, right):
    return lax.dot_general(
        left, right, (((1,), (1,)), ((), ())), preferred_element_type=jnp.float32
    )


def swiglu_grads(normed_rows, gate_pre, up_proj, grad_hidden):
    sigmoid_g = jax.nn.sigmoid(gate_pre)
    grad_gate_pre = (
        grad_hidden * up_proj * sigmoid_g * (1.0 + gate_pre * (1.0 - sigmoid_g))
    ).astype(jnp.bfloat16)
    grad_up = (grad_hidden * gate_pre * sigmoid_g).astype(jnp.bfloat16)
    grad_gate_up = jnp.stack(
        [contract_rows(normed_rows, grad_gate_pre), contract_rows(normed_rows, grad_up)]
    )
    return (grad_gate_pre, grad_up, grad_gate_up)


def per_device_body(
    tokens,
    segment_ids,
    gain_in,
    w_qkv,
    conv_w,
    w_decay,
    a_log,
    dt_bias,
    w_gate_o,
    gain_o,
    w_out,
    gain_mid,
    w_gate_up,
    w_down,
    cotangent,
):
    segments = segment_ids[0]
    residual_in = tokens.astype(jnp.float32)
    normed_f, norm_in_back = jax.vjp(rms_scale, residual_in, gain_in)
    normed_in = normed_f.astype(jnp.bfloat16)
    raw_proj = jnp.dot(normed_in, w_qkv, preferred_element_type=jnp.float32)
    gate_logits = jnp.dot(normed_in, w_decay, preferred_element_type=jnp.float32)
    out_gate = jnp.dot(normed_in, w_gate_o, preferred_element_type=jnp.float32)

    def local_mixer(raw_a, logit_a, gate_a, conv_a, log_a, bias_a, gain_a):
        return mixer(raw_a, logit_a, gate_a, segments, conv_a, log_a, bias_a, gain_a)

    mixed_f, mixer_back = jax.vjp(
        local_mixer, raw_proj, gate_logits, out_gate, conv_w, a_log, dt_bias, gain_o
    )
    mixed = mixed_f.astype(jnp.bfloat16)
    gate_up_rows, down_rows = (
        lax.all_gather(w_gate_up, "row", axis=1, tiled=True),
        lax.all_gather(w_down, "row", axis=1, tiled=True),
    )
    cot_all = lax.all_gather(cotangent, "col", axis=0, tiled=True)
    mixed, gate_up_rows, down_rows, cot_all = lax.optimization_barrier(
        (mixed, gate_up_rows, down_rows, cot_all)
    )
    middle = residual_in + jnp.dot(mixed, w_out, preferred_element_type=jnp.float32)
    middle_out = lax.optimization_barrier(middle)
    normed_mf, norm_mid_back = jax.vjp(rms_scale, middle, gain_mid)
    normed_mid = normed_mf.astype(jnp.bfloat16)
    normed_all = lax.all_gather(normed_mid, "col", axis=0, tiled=True)
    gate_pre = jnp.dot(normed_all, gate_up_rows[0], preferred_element_type=jnp.float32)
    up_proj = jnp.dot(normed_all, gate_up_rows[1], preferred_element_type=jnp.float32)
    hidden = (jax.nn.silu(gate_pre) * up_proj).astype(jnp.bfloat16)
    ffn_part = jnp.dot(hidden, down_rows, preferred_element_type=jnp.float32).astype(jnp.bfloat16)
    grad_hidden = contract_cols(cot_all, down_rows)
    grad_gate_pre, grad_up, grad_gu_part = swiglu_grads(normed_all, gate_pre, up_proj, grad_hidden)
    grad_down_part = contract_rows(hidden, cot_all)
    grad_nm_part = (
        contract_cols(grad_gate_pre, gate_up_rows[0]) + contract_cols(grad_up, gate_up_rows[1])
    ).astype(jnp.bfloat16)
    grad_normed_mid = lax.psum_scatter(grad_nm_part, "col", scatter_dimension=0, tiled=True)
    grad_normed_mid = grad_normed_mid.astype(jnp.float32)
    ffn_out = summed_by_exchange(ffn_part, "col", 0)
    grad_gate_up, grad_down = (
        summed_by_exchange(grad_gu_part.astype(jnp.bfloat16), "row", 1),
        summed_by_exchange(grad_down_part.astype(jnp.bfloat16), "row", 1),
    )
    grad_mid_norm, grad_gain_mid = norm_mid_back(grad_normed_mid)
    grad_middle = cotangent.astype(jnp.float32) + grad_mid_norm
    grad_middle_b = grad_middle.astype(jnp.bfloat16)
    grad_out = contract_rows(mixed, grad_middle_b)
    grad_mixed = contract_cols(grad_middle_b, w_out)
    grad_raw, grad_logits, grad_gate_out, grad_conv, grad_a_log, grad_dt_bias, grad_gain_o = (
        mixer_back(grad_mixed)
    )
    grad_raw_b = grad_raw.astype(jnp.bfloat16)
    grad_logits_b = grad_logits.astype(jnp.bfloat16)
    grad_gate_b = grad_gate_out.astype(jnp.bfloat16)
    grad_qkv = contract_rows(normed_in, grad_raw_b)
    grad_decay = contract_rows(normed_in, grad_logits_b)
    grad_gate_o = contract_rows(normed_in, grad_gate_b)
    early = summed_bf16((grad_out, grad_gate_o))
    block_out = (middle_out + ffn_out).astype(jnp.bfloat16)
    grad_normed_in = (
        contract_cols(grad_raw_b, w_qkv)
        + contract_cols(grad_logits_b, w_decay)
        + contract_cols(grad_gate_b, w_gate_o)
    )
    grad_in_norm, grad_gain_in = norm_in_back(grad_normed_in)
    grad_tokens = grad_middle + grad_in_norm
    late = summed_bf16((grad_qkv,), after=early[0])
    small = summed_f32(
        (grad_gain_in, grad_conv, grad_decay, grad_a_log, grad_dt_bias, grad_gain_o, grad_gain_mid)
    )
    return (
        block_out,
        grad_tokens,
        small[0],
        late[0],
        small[1],
        small[2],
        small[3],
        small[4],
        early[1],
        small[5],
        early[0],
        small[6],
        grad_gate_up,
        grad_down,
    )


def summed_by_exchange(part, axis, dim):
    n = lax.axis_size(axis)
    shape = part.shape
    pieces = part.reshape(shape[:dim] + (n, shape[dim] // n) + shape[dim + 1 :])
    got = lax.all_to_all(pieces, axis, dim, dim, tiled=False)
    return jnp.sum(got.astype(jnp.float32), axis=dim)


def split_flat(total, parts):
    out, at = [], 0
    for p in parts:
        out.append(total[at : at + p.size].reshape(p.shape).astype(jnp.float32))
        at += p.size
    return out


def summed_f32(parts):
    flat = jnp.concatenate([p.reshape(-1) for p in parts])
    for axis in ("col", "row"):
        n = lax.axis_size(axis)
        if n & (n - 1):
            flat = lax.psum(flat, axis)
            continue
        step = 1
        while step < n:
            flat = flat + lax.ppermute(flat, axis, [(i, i ^ step) for i in range(n)])
            step *= 2
    return split_flat(flat, parts)


def summed_bf16(parts, after=None):
    flat = jnp.concatenate([p.astype(jnp.bfloat16).reshape(-1) for p in parts])
    if after is not None:
        flat, _ = lax.optimization_barrier((flat, after))
    return split_flat(lax.psum(flat, ("row", "col")), parts)


def solution(mesh):
    in_specs = (
        P(("row", "col"), None),
        P(("row", "col"), None),
        P(),
        P(),
        P(),
        P(),
        P(),
        P(),
        P(),
        P(),
        P(),
        P(),
        P(None, "row", "col"),
        P("col", "row"),
        P(("row", "col"), None),
    )
    out_specs = (
        P(("row", "col"), None),
        P(("row", "col"), None),
        P(),
        P(),
        P(),
        P(),
        P(),
        P(),
        P(),
        P(),
        P(),
        P(),
        P(None, "row", "col"),
        P("col", "row"),
    )
    return jax.shard_map(
        per_device_body, mesh=mesh, in_specs=in_specs, out_specs=out_specs, check_vma=False
    )
```

```python
import jax
import jax.numpy as jnp
from jax import lax
from jax.sharding import PartitionSpec as P

HEADS = 6
HEAD_K = 128
HEAD_V = 256
CONV = 4
STRETCH = 64
HI = lax.Precision.HIGHEST


EPSILON = 1e-06


def rms_scale(values, gain_vec):
    return (
        values * lax.rsqrt(jnp.mean(values * values, axis=-1, keepdims=True) + EPSILON) * gain_vec
    )


def conv_silu(raw_proj, conv_weight, segments):
    length = raw_proj.shape[0]
    mixed = raw_proj * conv_weight[CONV - 1]
    for offset in range(1, CONV):
        shifted = jnp.concatenate(
            [jnp.zeros((offset, raw_proj.shape[1]), jnp.float32), raw_proj[: length - offset]],
            axis=0,
        )
        seg_shifted = jnp.concatenate(
            [jnp.full((offset,), -1, jnp.int32), segments[: length - offset]], axis=0
        )
        keep_tap = (seg_shifted == segments).astype(jnp.float32)[:, None]
        mixed = mixed + shifted * keep_tap * conv_weight[CONV - 1 - offset]
    return jax.nn.silu(mixed)


def head_blocks(array, stretch_count):
    shaped = array.reshape((stretch_count, STRETCH) + array.shape[1:])
    return jnp.swapaxes(shaped, 1, 2)


LEAF = 8


def _mm(a, b):
    return jnp.einsum("...ij,...jk->...ik", a, b, precision=HI)


def _unit_lower_inverse_fwd_impl(strict_part):
    n = strict_part.shape[-1]
    nb = n // LEAF
    eye = jnp.eye(LEAF, dtype=strict_part.dtype)
    diag = jnp.stack(
        [strict_part[..., i * LEAF:(i + 1) * LEAF, i * LEAF:(i + 1) * LEAF] for i in range(nb)], axis=-3
    )
    sq = _mm(diag, diag)
    blocks = _mm(_mm(eye - diag, eye + sq), eye + _mm(sq, sq))
    size = LEAF
    while size < n:
        count = n // (2 * size)
        upper_inv = blocks[..., 0::2, :, :]
        lower_inv = blocks[..., 1::2, :, :]
        cross = jnp.stack(
            [strict_part[..., (2 * p + 1) * size:(2 * p + 2) * size, 2 * p * size:(2 * p + 1) * size] for p in range(count)],
            axis=-3,
        )
        corner = -_mm(lower_inv, _mm(cross, upper_inv))
        zeros = jnp.zeros_like(corner)
        top = jnp.concatenate([upper_inv, zeros], axis=-1)
        bottom = jnp.concatenate([corner, lower_inv], axis=-1)
        blocks = jnp.concatenate([top, bottom], axis=-2)
        size *= 2
    return blocks[..., 0, :, :]


@jax.custom_vjp
def unit_lower_inverse(strict_part):
    return _unit_lower_inverse_fwd_impl(strict_part)


def _uli_fwd(strict_part):
    inv = _unit_lower_inverse_fwd_impl(strict_part)
    return inv, inv


def _uli_bwd(inv, grad):
    n = inv.shape[-1]
    below = jnp.arange(n)[:, None] > jnp.arange(n)[None, :]
    inv_t = jnp.swapaxes(inv, -1, -2)
    return (jnp.where(below, -_mm(inv_t, _mm(grad, inv_t)), 0.0),)


unit_lower_inverse.defvjp(_uli_fwd, _uli_bwd)


def delta_rule(queries, keys_unit, values_part, log_decay, write_rate, segments):
    length = queries.shape[0]
    nc = length // STRETCH
    q = head_blocks(queries, nc)
    k = head_blocks(keys_unit, nc)
    v = head_blocks(values_part, nc)
    g = head_blocks(log_decay, nc)
    beta = head_blocks(write_rate, nc)
    seg = segments.reshape(nc, STRETCH)
    seg_prev = jnp.concatenate([jnp.full((1,), -1, jnp.int32), seg[:-1, -1]], axis=0)
    row = jnp.arange(STRETCH)[:, None]
    col = jnp.arange(STRETCH)[None, :]
    cum = jnp.cumsum(g, axis=-1)
    live = ((seg[:, :, None] == seg[:, None, :]) & (row >= col))[:, None]
    gap = cum[..., :, None] - cum[..., None, :]
    decay_mat = jnp.where(live, jnp.exp(jnp.where(live, gap, 0.0)), 0.0)
    carry = jnp.exp(cum) * (seg == seg_prev[:, None]).astype(jnp.float32)[:, None, :]
    gram = jnp.einsum("nhck,nhsk->nhcs", k, k, precision=HI)
    strict = jnp.where((row > col)[None, None], decay_mat, 0.0)
    inverse = unit_lower_inverse(beta[..., None] * strict * gram)
    rhs = jnp.concatenate([beta[..., None] * v, (beta * carry)[..., None] * k], axis=-1)
    sol = jnp.einsum("nhcs,nhsv->nhcv", inverse, rhs, precision=HI)
    u, w = sol[..., :HEAD_V], sol[..., HEAD_V:]
    kw = k * decay_mat[..., -1, :, None]
    m = jnp.einsum("nhck,nhcj->nhkj", kw, w, precision=HI)
    nn = jnp.einsum("nhck,nhcv->nhkv", kw, u, precision=HI)
    a_last = carry[..., -1]
    states = [jnp.zeros((HEADS, HEAD_K, HEAD_V), jnp.float32)]
    s = nn[0]
    states.append(s)
    for c in range(1, nc - 1):
        s = a_last[c][:, None, None] * s - jnp.einsum("hkj,hjv->hkv", m[c], s, precision=HI) + nn[c]
        states.append(s)
    st = jnp.stack(states)
    p = u - jnp.einsum("nhck,nhkv->nhcv", w, st, precision=HI)
    scores = jnp.einsum("nhck,nhsk->nhcs", q, k, precision=HI) * decay_mat
    out = carry[..., None] * jnp.einsum("nhck,nhkv->nhcv", q, st, precision=HI)
    out = out + jnp.einsum("nhcs,nhsv->nhcv", scores, p, precision=HI)
    return jnp.swapaxes(out, 1, 2).reshape(length, HEADS, HEAD_V)


def mixer_core(raw_proj, gate_logits, segments, conv_weight, a_log, dt_bias):
    length = raw_proj.shape[0]
    key_dim = HEADS * HEAD_K
    conv = conv_silu(raw_proj, conv_weight, segments)
    queries = conv[:, :key_dim].reshape(length, HEADS, HEAD_K)
    keys_raw = conv[:, key_dim : 2 * key_dim].reshape(length, HEADS, HEAD_K)
    values_part = conv[:, 2 * key_dim :].reshape(length, HEADS, HEAD_V)
    queries = (
        queries
        * lax.rsqrt(jnp.sum(queries * queries, axis=-1, keepdims=True) + EPSILON)
        * HEAD_K ** (-0.5)
    )
    keys_unit = keys_raw * lax.rsqrt(jnp.sum(keys_raw * keys_raw, axis=-1, keepdims=True) + EPSILON)
    log_decay = -jnp.exp(a_log) * jax.nn.softplus(gate_logits[:, :HEADS] + dt_bias)
    write_rate = jax.nn.sigmoid(gate_logits[:, HEADS:])
    return delta_rule(queries, keys_unit, values_part, log_decay, write_rate, segments)


def out_norm(delta_out, out_gate, gain_o):
    length = delta_out.shape[0]
    gate_vals = jax.nn.silu(out_gate).reshape(length, HEADS, HEAD_V)
    normed = (
        delta_out
        * lax.rsqrt(jnp.mean(delta_out * delta_out, axis=-1, keepdims=True) + EPSILON)
        * gain_o
        * gate_vals
    )
    return normed.reshape(length, HEADS * HEAD_V)


def contract_rows(left, right):
    return lax.dot_general(
        left, right, (((0,), (0,)), ((), ())), preferred_element_type=jnp.float32
    )


def contract_cols(left, right):
    return lax.dot_general(
        left, right, (((1,), (1,)), ((), ())), preferred_element_type=jnp.float32
    )


def swiglu_grads(normed_rows, gate_pre, up_proj, grad_hidden):
    sigmoid_g = jax.nn.sigmoid(gate_pre)
    grad_gate_pre = (
        grad_hidden * up_proj * sigmoid_g * (1.0 + gate_pre * (1.0 - sigmoid_g))
    ).astype(jnp.bfloat16)
    grad_up = (grad_hidden * gate_pre * sigmoid_g).astype(jnp.bfloat16)
    grad_gate_up = jnp.stack(
        [contract_rows(normed_rows, grad_gate_pre), contract_rows(normed_rows, grad_up)]
    )
    return (grad_gate_pre, grad_up, grad_gate_up)


def per_device_body(
    tokens,
    segment_ids,
    gain_in,
    w_qkv,
    conv_w,
    w_decay,
    a_log,
    dt_bias,
    w_gate_o,
    gain_o,
    w_out,
    gain_mid,
    w_gate_up,
    w_down,
    cotangent,
):
    segments = segment_ids[0]
    residual_in = tokens.astype(jnp.float32)
    normed_f, norm_in_back = jax.vjp(rms_scale, residual_in, gain_in)
    normed_in = normed_f.astype(jnp.bfloat16)
    raw_proj = jnp.dot(normed_in, w_qkv, preferred_element_type=jnp.float32)
    gate_logits = jnp.dot(normed_in, w_decay, preferred_element_type=jnp.float32)
    out_gate = jnp.dot(normed_in, w_gate_o, preferred_element_type=jnp.float32)

    def local_core(raw_a, logit_a, conv_a, log_a, bias_a):
        return mixer_core(raw_a, logit_a, segments, conv_a, log_a, bias_a)

    delta_out, core_back = jax.vjp(local_core, raw_proj, gate_logits, conv_w, a_log, dt_bias)
    mixed_f, out_norm_back = jax.vjp(out_norm, delta_out, out_gate, gain_o)
    mixed = mixed_f.astype(jnp.bfloat16)
    gate_up_rows, down_rows = (
        lax.all_gather(w_gate_up, "row", axis=1, tiled=True),
        lax.all_gather(w_down, "row", axis=1, tiled=True),
    )
    cot_all = lax.all_gather(cotangent, "col", axis=0, tiled=True)
    mixed, gate_up_rows, down_rows, cot_all = lax.optimization_barrier(
        (mixed, gate_up_rows, down_rows, cot_all)
    )
    middle = residual_in + jnp.dot(mixed, w_out, preferred_element_type=jnp.float32)
    middle_out = lax.optimization_barrier(middle)
    normed_mf, norm_mid_back = jax.vjp(rms_scale, middle, gain_mid)
    normed_mid = normed_mf.astype(jnp.bfloat16)
    normed_all = lax.all_gather(normed_mid, "col", axis=0, tiled=True)
    gate_pre = jnp.dot(normed_all, gate_up_rows[0], preferred_element_type=jnp.float32)
    up_proj = jnp.dot(normed_all, gate_up_rows[1], preferred_element_type=jnp.float32)
    hidden = (jax.nn.silu(gate_pre) * up_proj).astype(jnp.bfloat16)
    ffn_part = jnp.dot(hidden, down_rows, preferred_element_type=jnp.float32).astype(jnp.bfloat16)
    grad_hidden = contract_cols(cot_all, down_rows)
    grad_gate_pre, grad_up, grad_gu_part = swiglu_grads(normed_all, gate_pre, up_proj, grad_hidden)
    grad_down_part = contract_rows(hidden, cot_all)
    grad_nm_part = (
        contract_cols(grad_gate_pre, gate_up_rows[0]) + contract_cols(grad_up, gate_up_rows[1])
    ).astype(jnp.bfloat16)
    grad_normed_mid = lax.psum_scatter(grad_nm_part, "col", scatter_dimension=0, tiled=True)
    grad_normed_mid = grad_normed_mid.astype(jnp.float32)
    ffn_out = summed_by_exchange(ffn_part, "col", 0)
    grad_gate_up, grad_down = (
        summed_by_exchange(grad_gu_part.astype(jnp.bfloat16), "row", 1),
        summed_by_exchange(grad_down_part.astype(jnp.bfloat16), "row", 1),
    )
    grad_mid_norm, grad_gain_mid = norm_mid_back(grad_normed_mid)
    grad_middle = cotangent.astype(jnp.float32) + grad_mid_norm
    grad_middle_b = grad_middle.astype(jnp.bfloat16)
    grad_out = contract_rows(mixed, grad_middle_b)
    grad_mixed = contract_cols(grad_middle_b, w_out)
    grad_delta, grad_gate_out, grad_gain_o = out_norm_back(grad_mixed)
    grad_gate_b = grad_gate_out.astype(jnp.bfloat16)
    grad_gate_o = contract_rows(normed_in, grad_gate_b)
    early_parts = (grad_out, grad_gate_o)
    early_flat = flat_bf16(early_parts)
    early_flat, grad_delta = lax.optimization_barrier((early_flat, grad_delta))
    early_total = lax.psum(early_flat, ("row", "col"))
    early = split_flat(early_total, early_parts)
    grad_raw, grad_logits, grad_conv, grad_a_log, grad_dt_bias = core_back(grad_delta)
    grad_raw_b = grad_raw.astype(jnp.bfloat16)
    grad_logits_b = grad_logits.astype(jnp.bfloat16)
    grad_qkv = contract_rows(normed_in, grad_raw_b)
    grad_decay = contract_rows(normed_in, grad_logits_b)
    block_out = (middle_out + ffn_out).astype(jnp.bfloat16)
    grad_normed_in = (
        contract_cols(grad_raw_b, w_qkv)
        + contract_cols(grad_logits_b, w_decay)
        + contract_cols(grad_gate_b, w_gate_o)
    )
    grad_in_norm, grad_gain_in = norm_in_back(grad_normed_in)
    grad_tokens = grad_middle + grad_in_norm
    late = summed_bf16((grad_qkv,), after=early[0])
    small = summed_f32(
        (grad_gain_in, grad_conv, grad_decay, grad_a_log, grad_dt_bias, grad_gain_o, grad_gain_mid)
    )
    return (
        block_out,
        grad_tokens,
        small[0],
        late[0],
        small[1],
        small[2],
        small[3],
        small[4],
        early[1],
        small[5],
        early[0],
        small[6],
        grad_gate_up,
        grad_down,
    )


def summed_by_exchange(part, axis, dim):
    n = lax.axis_size(axis)
    shape = part.shape
    pieces = part.reshape(shape[:dim] + (n, shape[dim] // n) + shape[dim + 1 :])
    got = lax.all_to_all(pieces, axis, dim, dim, tiled=False)
    return jnp.sum(got.astype(jnp.float32), axis=dim)


def split_flat(total, parts):
    out, at = [], 0
    for p in parts:
        out.append(total[at : at + p.size].reshape(p.shape).astype(jnp.float32))
        at += p.size
    return out


def summed_f32(parts):
    flat = jnp.concatenate([p.reshape(-1) for p in parts])
    for axis in ("col", "row"):
        n = lax.axis_size(axis)
        if n & (n - 1):
            flat = lax.psum(flat, axis)
            continue
        step = 1
        while step < n:
            flat = flat + lax.ppermute(flat, axis, [(i, i ^ step) for i in range(n)])
            step *= 2
    return split_flat(flat, parts)


def flat_bf16(parts):
    return jnp.concatenate([p.astype(jnp.bfloat16).reshape(-1) for p in parts])


def summed_bf16(parts, after=None):
    flat = flat_bf16(parts)
    if after is not None:
        flat, _ = lax.optimization_barrier((flat, after))
    return split_flat(lax.psum(flat, ("row", "col")), parts)


def solution(mesh):
    in_specs = (
        P(("row", "col"), None),
        P(("row", "col"), None),
        P(),
        P(),
        P(),
        P(),
        P(),
        P(),
        P(),
        P(),
        P(),
        P(),
        P(None, "row", "col"),
        P("col", "row"),
        P(("row", "col"), None),
    )
    out_specs = (
        P(("row", "col"), None),
        P(("row", "col"), None),
        P(),
        P(),
        P(),
        P(),
        P(),
        P(),
        P(),
        P(),
        P(),
        P(),
        P(None, "row", "col"),
        P("col", "row"),
    )
    return jax.shard_map(
        per_device_body, mesh=mesh, in_specs=in_specs, out_specs=out_specs, check_vma=False
    )
```

```python
import jax
import jax.numpy as jnp
from jax import lax
from jax.sharding import PartitionSpec as P

HEADS = 6
HEAD_K = 128
HEAD_V = 256
CONV = 4
STRETCH = 64
HI = lax.Precision.HIGHEST


EPSILON = 1e-06


def rms_scale(values, gain_vec):
    return (
        values * lax.rsqrt(jnp.mean(values * values, axis=-1, keepdims=True) + EPSILON) * gain_vec
    )


def conv_silu(raw_proj, conv_weight, segments):
    length = raw_proj.shape[0]
    mixed = raw_proj * conv_weight[CONV - 1]
    for offset in range(1, CONV):
        shifted = jnp.concatenate(
            [jnp.zeros((offset, raw_proj.shape[1]), jnp.float32), raw_proj[: length - offset]],
            axis=0,
        )
        seg_shifted = jnp.concatenate(
            [jnp.full((offset,), -1, jnp.int32), segments[: length - offset]], axis=0
        )
        keep_tap = (seg_shifted == segments).astype(jnp.float32)[:, None]
        mixed = mixed + shifted * keep_tap * conv_weight[CONV - 1 - offset]
    return jax.nn.silu(mixed)


def head_blocks(array, stretch_count):
    shaped = array.reshape((stretch_count, STRETCH) + array.shape[1:])
    return jnp.swapaxes(shaped, 1, 2)


LEAF = 8


def _mm(a, b):
    return jnp.einsum("...ij,...jk->...ik", a, b, precision=HI)


def _unit_lower_inverse_fwd_impl(strict_part):
    n = strict_part.shape[-1]
    nb = n // LEAF
    eye = jnp.eye(LEAF, dtype=strict_part.dtype)
    diag = jnp.stack(
        [strict_part[..., i * LEAF:(i + 1) * LEAF, i * LEAF:(i + 1) * LEAF] for i in range(nb)], axis=-3
    )
    sq = _mm(diag, diag)
    blocks = _mm(_mm(eye - diag, eye + sq), eye + _mm(sq, sq))
    size = LEAF
    while size < n:
        count = n // (2 * size)
        upper_inv = blocks[..., 0::2, :, :]
        lower_inv = blocks[..., 1::2, :, :]
        cross = jnp.stack(
            [strict_part[..., (2 * p + 1) * size:(2 * p + 2) * size, 2 * p * size:(2 * p + 1) * size] for p in range(count)],
            axis=-3,
        )
        corner = -_mm(lower_inv, _mm(cross, upper_inv))
        zeros = jnp.zeros_like(corner)
        top = jnp.concatenate([upper_inv, zeros], axis=-1)
        bottom = jnp.concatenate([corner, lower_inv], axis=-1)
        blocks = jnp.concatenate([top, bottom], axis=-2)
        size *= 2
    return blocks[..., 0, :, :]


@jax.custom_vjp
def unit_lower_inverse(strict_part):
    return _unit_lower_inverse_fwd_impl(strict_part)


def _uli_fwd(strict_part):
    inv = _unit_lower_inverse_fwd_impl(strict_part)
    return inv, inv


def _uli_bwd(inv, grad):
    n = inv.shape[-1]
    below = jnp.arange(n)[:, None] > jnp.arange(n)[None, :]
    inv_t = jnp.swapaxes(inv, -1, -2)
    return (jnp.where(below, -_mm(inv_t, _mm(grad, inv_t)), 0.0),)


unit_lower_inverse.defvjp(_uli_fwd, _uli_bwd)


def delta_rule(queries, keys_unit, values_part, log_decay, write_rate, segments):
    length = queries.shape[0]
    nc = length // STRETCH
    q = head_blocks(queries, nc)
    k = head_blocks(keys_unit, nc)
    v = head_blocks(values_part, nc)
    g = head_blocks(log_decay, nc)
    beta = head_blocks(write_rate, nc)
    seg = segments.reshape(nc, STRETCH)
    seg_prev = jnp.concatenate([jnp.full((1,), -1, jnp.int32), seg[:-1, -1]], axis=0)
    row = jnp.arange(STRETCH)[:, None]
    col = jnp.arange(STRETCH)[None, :]
    cum = jnp.cumsum(g, axis=-1)
    live = ((seg[:, :, None] == seg[:, None, :]) & (row >= col))[:, None]
    gap = cum[..., :, None] - cum[..., None, :]
    decay_mat = jnp.where(live, jnp.exp(jnp.where(live, gap, 0.0)), 0.0)
    carry = jnp.exp(cum) * (seg == seg_prev[:, None]).astype(jnp.float32)[:, None, :]
    gram = jnp.einsum("nhck,nhsk->nhcs", k, k, precision=HI)
    strict = jnp.where((row > col)[None, None], decay_mat, 0.0)
    inverse = unit_lower_inverse(beta[..., None] * strict * gram)
    rhs = jnp.concatenate([beta[..., None] * v, (beta * carry)[..., None] * k], axis=-1)
    sol = jnp.einsum("nhcs,nhsv->nhcv", inverse, rhs, precision=HI)
    u, w = sol[..., :HEAD_V], sol[..., HEAD_V:]
    kw = k * decay_mat[..., -1, :, None]
    m = jnp.einsum("nhck,nhcj->nhkj", kw, w, precision=HI)
    nn = jnp.einsum("nhck,nhcv->nhkv", kw, u, precision=HI)
    a_last = carry[..., -1]
    states = [jnp.zeros((HEADS, HEAD_K, HEAD_V), jnp.float32)]
    s = nn[0]
    states.append(s)
    for c in range(1, nc - 1):
        s = a_last[c][:, None, None] * s - jnp.einsum("hkj,hjv->hkv", m[c], s, precision=HI) + nn[c]
        states.append(s)
    st = jnp.stack(states)
    p = u - jnp.einsum("nhck,nhkv->nhcv", w, st, precision=HI)
    scores = jnp.einsum("nhck,nhsk->nhcs", q, k, precision=HI) * decay_mat
    out = carry[..., None] * jnp.einsum("nhck,nhkv->nhcv", q, st, precision=HI)
    out = out + jnp.einsum("nhcs,nhsv->nhcv", scores, p, precision=HI)
    return jnp.swapaxes(out, 1, 2).reshape(length, HEADS, HEAD_V)


def mixer_core(raw_proj, gate_logits, segments, conv_weight, a_log, dt_bias):
    length = raw_proj.shape[0]
    key_dim = HEADS * HEAD_K
    conv = conv_silu(raw_proj, conv_weight, segments)
    queries = conv[:, :key_dim].reshape(length, HEADS, HEAD_K)
    keys_raw = conv[:, key_dim : 2 * key_dim].reshape(length, HEADS, HEAD_K)
    values_part = conv[:, 2 * key_dim :].reshape(length, HEADS, HEAD_V)
    queries = (
        queries
        * lax.rsqrt(jnp.sum(queries * queries, axis=-1, keepdims=True) + EPSILON)
        * HEAD_K ** (-0.5)
    )
    keys_unit = keys_raw * lax.rsqrt(jnp.sum(keys_raw * keys_raw, axis=-1, keepdims=True) + EPSILON)
    log_decay = -jnp.exp(a_log) * jax.nn.softplus(gate_logits[:, :HEADS] + dt_bias)
    write_rate = jax.nn.sigmoid(gate_logits[:, HEADS:])
    return delta_rule(queries, keys_unit, values_part, log_decay, write_rate, segments)


def out_norm(delta_out, out_gate, gain_o):
    length = delta_out.shape[0]
    gate_vals = jax.nn.silu(out_gate).reshape(length, HEADS, HEAD_V)
    normed = (
        delta_out
        * lax.rsqrt(jnp.mean(delta_out * delta_out, axis=-1, keepdims=True) + EPSILON)
        * gain_o
        * gate_vals
    )
    return normed.reshape(length, HEADS * HEAD_V)


def contract_rows(left, right):
    return lax.dot_general(
        left, right, (((0,), (0,)), ((), ())), preferred_element_type=jnp.float32
    )


def contract_cols(left, right):
    return lax.dot_general(
        left, right, (((1,), (1,)), ((), ())), preferred_element_type=jnp.float32
    )


def swiglu_grads(normed_rows, gate_pre, up_proj, grad_hidden):
    sigmoid_g = jax.nn.sigmoid(gate_pre)
    grad_gate_pre = (
        grad_hidden * up_proj * sigmoid_g * (1.0 + gate_pre * (1.0 - sigmoid_g))
    ).astype(jnp.bfloat16)
    grad_up = (grad_hidden * gate_pre * sigmoid_g).astype(jnp.bfloat16)
    grad_gate_up = jnp.stack(
        [contract_rows(normed_rows, grad_gate_pre), contract_rows(normed_rows, grad_up)]
    )
    return (grad_gate_pre, grad_up, grad_gate_up)


def per_device_body(
    tokens,
    segment_ids,
    gain_in,
    w_qkv,
    conv_w,
    w_decay,
    a_log,
    dt_bias,
    w_gate_o,
    gain_o,
    w_out,
    gain_mid,
    w_gate_up,
    w_down,
    cotangent,
):
    segments = segment_ids[0]
    residual_in = tokens.astype(jnp.float32)
    normed_f, norm_in_back = jax.vjp(rms_scale, residual_in, gain_in)
    normed_in = normed_f.astype(jnp.bfloat16)
    raw_proj = jnp.dot(normed_in, w_qkv, preferred_element_type=jnp.float32)
    gate_logits = jnp.dot(normed_in, w_decay, preferred_element_type=jnp.float32)
    out_gate = jnp.dot(normed_in, w_gate_o, preferred_element_type=jnp.float32)

    def local_core(raw_a, logit_a, conv_a, log_a, bias_a):
        return mixer_core(raw_a, logit_a, segments, conv_a, log_a, bias_a)

    delta_out, core_back = jax.vjp(local_core, raw_proj, gate_logits, conv_w, a_log, dt_bias)
    mixed_f, out_norm_back = jax.vjp(out_norm, delta_out, out_gate, gain_o)
    mixed = mixed_f.astype(jnp.bfloat16)
    stacked = jnp.concatenate([w_gate_up, w_down.T[None]], axis=0)
    stacked_rows = lax.all_gather(stacked, "row", axis=1, tiled=True)
    gate_up_rows, down_rows = stacked_rows[:2], stacked_rows[2].T
    cot_all = lax.all_gather(cotangent, "col", axis=0, tiled=True)
    mixed, gate_up_rows, down_rows, cot_all = lax.optimization_barrier(
        (mixed, gate_up_rows, down_rows, cot_all)
    )
    middle = residual_in + jnp.dot(mixed, w_out, preferred_element_type=jnp.float32)
    middle_out = lax.optimization_barrier(middle)
    normed_mf, norm_mid_back = jax.vjp(rms_scale, middle, gain_mid)
    normed_mid = normed_mf.astype(jnp.bfloat16)
    normed_all = lax.all_gather(normed_mid, "col", axis=0, tiled=True)
    gate_pre = jnp.dot(normed_all, gate_up_rows[0], preferred_element_type=jnp.float32)
    up_proj = jnp.dot(normed_all, gate_up_rows[1], preferred_element_type=jnp.float32)
    hidden = (jax.nn.silu(gate_pre) * up_proj).astype(jnp.bfloat16)
    ffn_part = jnp.dot(hidden, down_rows, preferred_element_type=jnp.float32).astype(jnp.bfloat16)
    grad_hidden = contract_cols(cot_all, down_rows)
    grad_gate_pre, grad_up, grad_gu_part = swiglu_grads(normed_all, gate_pre, up_proj, grad_hidden)
    grad_down_part = contract_rows(hidden, cot_all)
    grad_nm_part = (
        contract_cols(grad_gate_pre, gate_up_rows[0]) + contract_cols(grad_up, gate_up_rows[1])
    ).astype(jnp.bfloat16)
    grad_normed_mid = lax.psum_scatter(grad_nm_part, "col", scatter_dimension=0, tiled=True)
    grad_normed_mid = grad_normed_mid.astype(jnp.float32)
    ffn_out = summed_by_exchange(ffn_part, "col", 0)
    grad_gate_up, grad_down = (
        summed_by_exchange(grad_gu_part.astype(jnp.bfloat16), "row", 1),
        summed_by_exchange(grad_down_part.astype(jnp.bfloat16), "row", 1),
    )
    grad_mid_norm, grad_gain_mid = norm_mid_back(grad_normed_mid)
    grad_middle = cotangent.astype(jnp.float32) + grad_mid_norm
    grad_middle_b = grad_middle.astype(jnp.bfloat16)
    grad_out = contract_rows(mixed, grad_middle_b)
    grad_mixed = contract_cols(grad_middle_b, w_out)
    grad_delta, grad_gate_out, grad_gain_o = out_norm_back(grad_mixed)
    grad_gate_b = grad_gate_out.astype(jnp.bfloat16)
    grad_gate_o = contract_rows(normed_in, grad_gate_b)
    early_b = (grad_out.astype(jnp.bfloat16), grad_gate_o.astype(jnp.bfloat16))
    early_b, grad_delta = lax.optimization_barrier((early_b, grad_delta))
    early_b = lax.psum(early_b, ("row", "col"))
    early = [e.astype(jnp.float32) for e in early_b]
    grad_raw, grad_logits, grad_conv, grad_a_log, grad_dt_bias = core_back(grad_delta)
    grad_raw_b = grad_raw.astype(jnp.bfloat16)
    grad_logits_b = grad_logits.astype(jnp.bfloat16)
    grad_qkv = contract_rows(normed_in, grad_raw_b)
    grad_decay = contract_rows(normed_in, grad_logits_b)
    grad_normed_in = (
        contract_cols(grad_raw_b, w_qkv)
        + contract_cols(grad_logits_b, w_decay)
        + contract_cols(grad_gate_b, w_gate_o)
    )
    grad_in_norm, grad_gain_in = norm_in_back(grad_normed_in)
    grad_tokens = grad_middle + grad_in_norm
    qkv_b, _, ffn_out = lax.optimization_barrier((grad_qkv.astype(jnp.bfloat16), early_b, ffn_out))
    block_out = (middle_out + ffn_out).astype(jnp.bfloat16)
    half = qkv_b.shape[1] // 2
    late = [
        jnp.concatenate(
            [
                lax.psum(qkv_b[:, :half], ("row", "col")).astype(jnp.float32),
                summed_all_by_exchange(qkv_b[:, half:]),
            ],
            axis=1,
        )
    ]
    small = summed_f32(
        (grad_gain_in, grad_conv, grad_decay, grad_a_log, grad_dt_bias, grad_gain_o, grad_gain_mid)
    )
    return (
        block_out,
        grad_tokens,
        small[0],
        late[0],
        small[1],
        small[2],
        small[3],
        small[4],
        early[1],
        small[5],
        early[0],
        small[6],
        grad_gate_up,
        grad_down,
    )


def summed_by_exchange(part, axis, dim):
    n = lax.axis_size(axis)
    shape = part.shape
    pieces = part.reshape(shape[:dim] + (n, shape[dim] // n) + shape[dim + 1 :])
    got = lax.all_to_all(pieces, axis, dim, dim, tiled=False)
    return jnp.sum(got.astype(jnp.float32), axis=dim)


def summed_all_by_exchange(part):
    axes = ("row", "col")
    n = lax.axis_size(axes)
    rows = part.shape[0]
    pieces = part.reshape((n, rows // n) + part.shape[1:])
    mine = jnp.sum(lax.all_to_all(pieces, axes, 0, 0).astype(jnp.float32), axis=0)
    shared = jnp.broadcast_to(mine.astype(jnp.bfloat16)[None], pieces.shape)
    return lax.all_to_all(shared, axes, 0, 0).reshape(part.shape).astype(jnp.float32)


def split_flat(total, parts):
    out, at = [], 0
    for p in parts:
        out.append(total[at : at + p.size].reshape(p.shape).astype(jnp.float32))
        at += p.size
    return out


def summed_f32(parts):
    flat = jnp.concatenate([p.reshape(-1) for p in parts])
    for axis in ("col", "row"):
        n = lax.axis_size(axis)
        if n & (n - 1):
            flat = lax.psum(flat, axis)
            continue
        step = 1
        while step < n:
            flat = flat + lax.ppermute(flat, axis, [(i, i ^ step) for i in range(n)])
            step *= 2
    return split_flat(flat, parts)


def solution(mesh):
    in_specs = (
        P(("row", "col"), None),
        P(("row", "col"), None),
        P(),
        P(),
        P(),
        P(),
        P(),
        P(),
        P(),
        P(),
        P(),
        P(),
        P(None, "row", "col"),
        P("col", "row"),
        P(("row", "col"), None),
    )
    out_specs = (
        P(("row", "col"), None),
        P(("row", "col"), None),
        P(),
        P(),
        P(),
        P(),
        P(),
        P(),
        P(),
        P(),
        P(),
        P(),
        P(None, "row", "col"),
        P("col", "row"),
    )
    return jax.shard_map(
        per_device_body, mesh=mesh, in_specs=in_specs, out_specs=out_specs, check_vma=False
    )
```

```python
import jax
import jax.numpy as jnp
from jax import lax
from jax.sharding import PartitionSpec as P

HEADS = 6
HEAD_K = 128
HEAD_V = 256
CONV = 4
STRETCH = 64
HI = lax.Precision.HIGHEST


EPSILON = 1e-06


def rms_scale(values, gain_vec):
    return (
        values * lax.rsqrt(jnp.mean(values * values, axis=-1, keepdims=True) + EPSILON) * gain_vec
    )


def conv_silu(raw_proj, conv_weight, segments):
    length = raw_proj.shape[0]
    mixed = raw_proj * conv_weight[CONV - 1]
    for offset in range(1, CONV):
        shifted = jnp.concatenate(
            [jnp.zeros((offset, raw_proj.shape[1]), jnp.float32), raw_proj[: length - offset]],
            axis=0,
        )
        seg_shifted = jnp.concatenate(
            [jnp.full((offset,), -1, jnp.int32), segments[: length - offset]], axis=0
        )
        keep_tap = (seg_shifted == segments).astype(jnp.float32)[:, None]
        mixed = mixed + shifted * keep_tap * conv_weight[CONV - 1 - offset]
    return jax.nn.silu(mixed)


def head_blocks(array, stretch_count):
    shaped = array.reshape((stretch_count, STRETCH) + array.shape[1:])
    return jnp.swapaxes(shaped, 1, 2)


LEAF = 8


def _mm(a, b):
    return jnp.einsum("...ij,...jk->...ik", a, b, precision=HI)


def _unit_lower_inverse_fwd_impl(strict_part):
    n = strict_part.shape[-1]
    nb = n // LEAF
    eye = jnp.eye(LEAF, dtype=strict_part.dtype)
    diag = jnp.stack(
        [strict_part[..., i * LEAF:(i + 1) * LEAF, i * LEAF:(i + 1) * LEAF] for i in range(nb)], axis=-3
    )
    sq = _mm(diag, diag)
    blocks = _mm(_mm(eye - diag, eye + sq), eye + _mm(sq, sq))
    size = LEAF
    while size < n:
        count = n // (2 * size)
        upper_inv = blocks[..., 0::2, :, :]
        lower_inv = blocks[..., 1::2, :, :]
        cross = jnp.stack(
            [strict_part[..., (2 * p + 1) * size:(2 * p + 2) * size, 2 * p * size:(2 * p + 1) * size] for p in range(count)],
            axis=-3,
        )
        corner = -_mm(lower_inv, _mm(cross, upper_inv))
        zeros = jnp.zeros_like(corner)
        top = jnp.concatenate([upper_inv, zeros], axis=-1)
        bottom = jnp.concatenate([corner, lower_inv], axis=-1)
        blocks = jnp.concatenate([top, bottom], axis=-2)
        size *= 2
    return blocks[..., 0, :, :]


@jax.custom_vjp
def unit_lower_inverse(strict_part):
    return _unit_lower_inverse_fwd_impl(strict_part)


def _uli_fwd(strict_part):
    inv = _unit_lower_inverse_fwd_impl(strict_part)
    return inv, inv


def _uli_bwd(inv, grad):
    n = inv.shape[-1]
    below = jnp.arange(n)[:, None] > jnp.arange(n)[None, :]
    inv_t = jnp.swapaxes(inv, -1, -2)
    return (jnp.where(below, -_mm(inv_t, _mm(grad, inv_t)), 0.0),)


unit_lower_inverse.defvjp(_uli_fwd, _uli_bwd)


def delta_rule(queries, keys_unit, values_part, log_decay, write_rate, segments):
    length = queries.shape[0]
    nc = length // STRETCH
    q = head_blocks(queries, nc)
    k = head_blocks(keys_unit, nc)
    v = head_blocks(values_part, nc)
    g = head_blocks(log_decay, nc)
    beta = head_blocks(write_rate, nc)
    seg = segments.reshape(nc, STRETCH)
    seg_prev = jnp.concatenate([jnp.full((1,), -1, jnp.int32), seg[:-1, -1]], axis=0)
    row = jnp.arange(STRETCH)[:, None]
    col = jnp.arange(STRETCH)[None, :]
    cum = jnp.cumsum(g, axis=-1)
    live = ((seg[:, :, None] == seg[:, None, :]) & (row >= col))[:, None]
    gap = cum[..., :, None] - cum[..., None, :]
    decay_mat = jnp.where(live, jnp.exp(jnp.where(live, gap, 0.0)), 0.0)
    carry = jnp.exp(cum) * (seg == seg_prev[:, None]).astype(jnp.float32)[:, None, :]
    gram = jnp.einsum("nhck,nhsk->nhcs", k, k, precision=HI)
    strict = jnp.where((row > col)[None, None], decay_mat, 0.0)
    inverse = unit_lower_inverse(beta[..., None] * strict * gram)
    rhs = jnp.concatenate([beta[..., None] * v, (beta * carry)[..., None] * k], axis=-1)
    sol = jnp.einsum("nhcs,nhsv->nhcv", inverse, rhs, precision=HI)
    u, w = sol[..., :HEAD_V], sol[..., HEAD_V:]
    kw = k * decay_mat[..., -1, :, None]
    m = jnp.einsum("nhck,nhcj->nhkj", kw, w, precision=HI)
    nn = jnp.einsum("nhck,nhcv->nhkv", kw, u, precision=HI)
    a_last = carry[..., -1]
    states = [jnp.zeros((HEADS, HEAD_K, HEAD_V), jnp.float32)]
    s = nn[0]
    states.append(s)
    for c in range(1, nc - 1):
        s = a_last[c][:, None, None] * s - jnp.einsum("hkj,hjv->hkv", m[c], s, precision=HI) + nn[c]
        states.append(s)
    st = jnp.stack(states)
    p = u - jnp.einsum("nhck,nhkv->nhcv", w, st, precision=HI)
    scores = jnp.einsum("nhck,nhsk->nhcs", q, k, precision=HI) * decay_mat
    out = carry[..., None] * jnp.einsum("nhck,nhkv->nhcv", q, st, precision=HI)
    out = out + jnp.einsum("nhcs,nhsv->nhcv", scores, p, precision=HI)
    return jnp.swapaxes(out, 1, 2).reshape(length, HEADS, HEAD_V)


def mixer_core(raw_proj, gate_logits, segments, conv_weight, a_log, dt_bias):
    length = raw_proj.shape[0]
    key_dim = HEADS * HEAD_K
    conv = conv_silu(raw_proj, conv_weight, segments)
    queries = conv[:, :key_dim].reshape(length, HEADS, HEAD_K)
    keys_raw = conv[:, key_dim : 2 * key_dim].reshape(length, HEADS, HEAD_K)
    values_part = conv[:, 2 * key_dim :].reshape(length, HEADS, HEAD_V)
    queries = (
        queries
        * lax.rsqrt(jnp.sum(queries * queries, axis=-1, keepdims=True) + EPSILON)
        * HEAD_K ** (-0.5)
    )
    keys_unit = keys_raw * lax.rsqrt(jnp.sum(keys_raw * keys_raw, axis=-1, keepdims=True) + EPSILON)
    log_decay = -jnp.exp(a_log) * jax.nn.softplus(gate_logits[:, :HEADS] + dt_bias)
    write_rate = jax.nn.sigmoid(gate_logits[:, HEADS:])
    return delta_rule(queries, keys_unit, values_part, log_decay, write_rate, segments)


def out_norm(delta_out, out_gate, gain_o):
    length = delta_out.shape[0]
    gate_vals = jax.nn.silu(out_gate).reshape(length, HEADS, HEAD_V)
    normed = (
        delta_out
        * lax.rsqrt(jnp.mean(delta_out * delta_out, axis=-1, keepdims=True) + EPSILON)
        * gain_o
        * gate_vals
    )
    return normed.reshape(length, HEADS * HEAD_V)


def contract_rows(left, right):
    return lax.dot_general(
        left, right, (((0,), (0,)), ((), ())), preferred_element_type=jnp.float32
    )


def contract_cols(left, right):
    return lax.dot_general(
        left, right, (((1,), (1,)), ((), ())), preferred_element_type=jnp.float32
    )


def swiglu_grads(normed_rows, gate_pre, up_proj, grad_hidden):
    sigmoid_g = jax.nn.sigmoid(gate_pre)
    grad_gate_pre = (
        grad_hidden * up_proj * sigmoid_g * (1.0 + gate_pre * (1.0 - sigmoid_g))
    ).astype(jnp.bfloat16)
    grad_up = (grad_hidden * gate_pre * sigmoid_g).astype(jnp.bfloat16)
    grad_gate_up = jnp.stack(
        [contract_rows(normed_rows, grad_gate_pre), contract_rows(normed_rows, grad_up)]
    )
    return (grad_gate_pre, grad_up, grad_gate_up)


def per_device_body(
    tokens,
    segment_ids,
    gain_in,
    w_qkv,
    conv_w,
    w_decay,
    a_log,
    dt_bias,
    w_gate_o,
    gain_o,
    w_out,
    gain_mid,
    w_gate_up,
    w_down,
    cotangent,
):
    segments = segment_ids[0]
    residual_in = tokens.astype(jnp.float32)
    normed_f, norm_in_back = jax.vjp(rms_scale, residual_in, gain_in)
    normed_in = normed_f.astype(jnp.bfloat16)
    raw_proj = jnp.dot(normed_in, w_qkv, preferred_element_type=jnp.float32)
    gate_logits = jnp.dot(normed_in, w_decay, preferred_element_type=jnp.float32)
    out_gate = jnp.dot(normed_in, w_gate_o, preferred_element_type=jnp.float32)

    def local_core(raw_a, logit_a, conv_a, log_a, bias_a):
        return mixer_core(raw_a, logit_a, segments, conv_a, log_a, bias_a)

    delta_out, core_back = jax.vjp(local_core, raw_proj, gate_logits, conv_w, a_log, dt_bias)
    mixed_f, out_norm_back = jax.vjp(out_norm, delta_out, out_gate, gain_o)
    mixed = mixed_f.astype(jnp.bfloat16)
    stacked = jnp.concatenate([w_gate_up, w_down.T[None]], axis=0)
    stacked_rows = lax.all_gather(stacked, "row", axis=1, tiled=True)
    gate_up_rows, down_rows = stacked_rows[:2], stacked_rows[2].T
    cot_all = lax.all_gather(cotangent, "col", axis=0, tiled=True)
    mixed, gate_up_rows, down_rows, cot_all = lax.optimization_barrier(
        (mixed, gate_up_rows, down_rows, cot_all)
    )
    middle = residual_in + jnp.dot(mixed, w_out, preferred_element_type=jnp.float32)
    middle_out = lax.optimization_barrier(middle)
    normed_mf, norm_mid_back = jax.vjp(rms_scale, middle, gain_mid)
    normed_mid = normed_mf.astype(jnp.bfloat16)
    normed_all = lax.all_gather(normed_mid, "col", axis=0, tiled=True)
    gate_pre = jnp.dot(normed_all, gate_up_rows[0], preferred_element_type=jnp.float32)
    up_proj = jnp.dot(normed_all, gate_up_rows[1], preferred_element_type=jnp.float32)
    hidden = (jax.nn.silu(gate_pre) * up_proj).astype(jnp.bfloat16)
    ffn_part = jnp.dot(hidden, down_rows, preferred_element_type=jnp.float32).astype(jnp.bfloat16)
    grad_hidden = contract_cols(cot_all, down_rows)
    grad_gate_pre, grad_up, grad_gu_part = swiglu_grads(normed_all, gate_pre, up_proj, grad_hidden)
    grad_down_part = contract_rows(hidden, cot_all)
    grad_nm_part = (
        contract_cols(grad_gate_pre, gate_up_rows[0]) + contract_cols(grad_up, gate_up_rows[1])
    ).astype(jnp.bfloat16)
    grad_normed_mid = lax.psum_scatter(grad_nm_part, "col", scatter_dimension=0, tiled=True)
    grad_normed_mid = grad_normed_mid.astype(jnp.float32)
    ffn_out = summed_by_exchange(ffn_part, "col", 0)
    grad_gate_up, grad_down = (
        summed_by_exchange(grad_gu_part.astype(jnp.bfloat16), "row", 1),
        summed_by_exchange(grad_down_part.astype(jnp.bfloat16), "row", 1),
    )
    grad_mid_norm, grad_gain_mid = norm_mid_back(grad_normed_mid)
    grad_middle = cotangent.astype(jnp.float32) + grad_mid_norm
    grad_middle_b = grad_middle.astype(jnp.bfloat16)
    grad_out = contract_rows(mixed, grad_middle_b)
    grad_mixed = contract_cols(grad_middle_b, w_out)
    grad_delta, grad_gate_out, grad_gain_o = out_norm_back(grad_mixed)
    grad_gate_b = grad_gate_out.astype(jnp.bfloat16)
    grad_gate_o = contract_rows(normed_in, grad_gate_b)
    early_b = (grad_out.astype(jnp.bfloat16), grad_gate_o.astype(jnp.bfloat16))
    early_b, grad_delta = lax.optimization_barrier((early_b, grad_delta))
    early_b = tuple(summed_in_two_steps(e) for e in early_b)
    early = [e.astype(jnp.float32) for e in early_b]
    grad_raw, grad_logits, grad_conv, grad_a_log, grad_dt_bias = core_back(grad_delta)
    grad_raw_b = grad_raw.astype(jnp.bfloat16)
    grad_logits_b = grad_logits.astype(jnp.bfloat16)
    grad_qkv = contract_rows(normed_in, grad_raw_b)
    grad_decay = contract_rows(normed_in, grad_logits_b)
    block_out = (middle_out + ffn_out).astype(jnp.bfloat16)
    grad_normed_in = (
        contract_cols(grad_raw_b, w_qkv)
        + contract_cols(grad_logits_b, w_decay)
        + contract_cols(grad_gate_b, w_gate_o)
    )
    grad_in_norm, grad_gain_in = norm_in_back(grad_normed_in)
    grad_tokens = grad_middle + grad_in_norm
    qkv_b, _ = lax.optimization_barrier((grad_qkv.astype(jnp.bfloat16), early_b))
    late = [summed_in_two_steps(qkv_b).astype(jnp.float32)]
    small = summed_f32(
        (grad_gain_in, grad_conv, grad_decay, grad_a_log, grad_dt_bias, grad_gain_o, grad_gain_mid)
    )
    return (
        block_out,
        grad_tokens,
        small[0],
        late[0],
        small[1],
        small[2],
        small[3],
        small[4],
        early[1],
        small[5],
        early[0],
        small[6],
        grad_gate_up,
        grad_down,
    )


def summed_by_exchange(part, axis, dim):
    n = lax.axis_size(axis)
    shape = part.shape
    pieces = part.reshape(shape[:dim] + (n, shape[dim] // n) + shape[dim + 1 :])
    got = lax.all_to_all(pieces, axis, dim, dim, tiled=False)
    return jnp.sum(got.astype(jnp.float32), axis=dim)


def summed_in_two_steps(part):
    axes = ("row", "col")
    mine = lax.psum_scatter(part, axes, scatter_dimension=0, tiled=True)
    return lax.all_gather(mine, axes, axis=0, tiled=True)


def split_flat(total, parts):
    out, at = [], 0
    for p in parts:
        out.append(total[at : at + p.size].reshape(p.shape).astype(jnp.float32))
        at += p.size
    return out


def summed_f32(parts):
    flat = jnp.concatenate([p.reshape(-1) for p in parts])
    for axis in ("col", "row"):
        n = lax.axis_size(axis)
        if n & (n - 1):
            flat = lax.psum(flat, axis)
            continue
        step = 1
        while step < n:
            flat = flat + lax.ppermute(flat, axis, [(i, i ^ step) for i in range(n)])
            step *= 2
    return split_flat(flat, parts)


def solution(mesh):
    in_specs = (
        P(("row", "col"), None),
        P(("row", "col"), None),
        P(),
        P(),
        P(),
        P(),
        P(),
        P(),
        P(),
        P(),
        P(),
        P(),
        P(None, "row", "col"),
        P("col", "row"),
        P(("row", "col"), None),
    )
    out_specs = (
        P(("row", "col"), None),
        P(("row", "col"), None),
        P(),
        P(),
        P(),
        P(),
        P(),
        P(),
        P(),
        P(),
        P(),
        P(),
        P(None, "row", "col"),
        P("col", "row"),
    )
    return jax.shard_map(
        per_device_body, mesh=mesh, in_specs=in_specs, out_specs=out_specs, check_vma=False
    )
```

```python
import jax
import jax.numpy as jnp
from jax import lax
from jax.sharding import PartitionSpec as P

HEADS = 6
HEAD_K = 128
HEAD_V = 256
CONV = 4
STRETCH = 64
HI = lax.Precision.HIGHEST


EPSILON = 1e-06


def rms_scale(values, gain_vec):
    return (
        values * lax.rsqrt(jnp.mean(values * values, axis=-1, keepdims=True) + EPSILON) * gain_vec
    )


def conv_silu(raw_proj, conv_weight, segments):
    length = raw_proj.shape[0]
    mixed = raw_proj * conv_weight[CONV - 1]
    for offset in range(1, CONV):
        shifted = jnp.concatenate(
            [jnp.zeros((offset, raw_proj.shape[1]), jnp.float32), raw_proj[: length - offset]],
            axis=0,
        )
        seg_shifted = jnp.concatenate(
            [jnp.full((offset,), -1, jnp.int32), segments[: length - offset]], axis=0
        )
        keep_tap = (seg_shifted == segments).astype(jnp.float32)[:, None]
        mixed = mixed + shifted * keep_tap * conv_weight[CONV - 1 - offset]
    return jax.nn.silu(mixed)


def head_blocks(array, stretch_count):
    shaped = array.reshape((stretch_count, STRETCH) + array.shape[1:])
    return jnp.swapaxes(shaped, 1, 2)


LEAF = 8


def _mm(a, b):
    return jnp.einsum("...ij,...jk->...ik", a, b, precision=HI)


def _unit_lower_inverse_fwd_impl(strict_part):
    n = strict_part.shape[-1]
    nb = n // LEAF
    eye = jnp.eye(LEAF, dtype=strict_part.dtype)
    diag = jnp.stack(
        [strict_part[..., i * LEAF:(i + 1) * LEAF, i * LEAF:(i + 1) * LEAF] for i in range(nb)], axis=-3
    )
    sq = _mm(diag, diag)
    blocks = _mm(_mm(eye - diag, eye + sq), eye + _mm(sq, sq))
    size = LEAF
    while size < n:
        count = n // (2 * size)
        upper_inv = blocks[..., 0::2, :, :]
        lower_inv = blocks[..., 1::2, :, :]
        cross = jnp.stack(
            [strict_part[..., (2 * p + 1) * size:(2 * p + 2) * size, 2 * p * size:(2 * p + 1) * size] for p in range(count)],
            axis=-3,
        )
        corner = -_mm(lower_inv, _mm(cross, upper_inv))
        zeros = jnp.zeros_like(corner)
        top = jnp.concatenate([upper_inv, zeros], axis=-1)
        bottom = jnp.concatenate([corner, lower_inv], axis=-1)
        blocks = jnp.concatenate([top, bottom], axis=-2)
        size *= 2
    return blocks[..., 0, :, :]


@jax.custom_vjp
def unit_lower_inverse(strict_part):
    return _unit_lower_inverse_fwd_impl(strict_part)


def _uli_fwd(strict_part):
    inv = _unit_lower_inverse_fwd_impl(strict_part)
    return inv, inv


def _uli_bwd(inv, grad):
    n = inv.shape[-1]
    below = jnp.arange(n)[:, None] > jnp.arange(n)[None, :]
    inv_t = jnp.swapaxes(inv, -1, -2)
    return (jnp.where(below, -_mm(inv_t, _mm(grad, inv_t)), 0.0),)


unit_lower_inverse.defvjp(_uli_fwd, _uli_bwd)


def delta_rule(queries, keys_unit, values_part, log_decay, write_rate, segments):
    length = queries.shape[0]
    nc = length // STRETCH
    q = head_blocks(queries, nc)
    k = head_blocks(keys_unit, nc)
    v = head_blocks(values_part, nc)
    g = head_blocks(log_decay, nc)
    beta = head_blocks(write_rate, nc)
    seg = segments.reshape(nc, STRETCH)
    seg_prev = jnp.concatenate([jnp.full((1,), -1, jnp.int32), seg[:-1, -1]], axis=0)
    row = jnp.arange(STRETCH)[:, None]
    col = jnp.arange(STRETCH)[None, :]
    cum = jnp.cumsum(g, axis=-1)
    live = ((seg[:, :, None] == seg[:, None, :]) & (row >= col))[:, None]
    gap = cum[..., :, None] - cum[..., None, :]
    decay_mat = jnp.where(live, jnp.exp(jnp.where(live, gap, 0.0)), 0.0)
    carry = jnp.exp(cum) * (seg == seg_prev[:, None]).astype(jnp.float32)[:, None, :]
    gram = jnp.einsum("nhck,nhsk->nhcs", k, k, precision=HI)
    strict = jnp.where((row > col)[None, None], decay_mat, 0.0)
    inverse = unit_lower_inverse(beta[..., None] * strict * gram)
    rhs = jnp.concatenate([beta[..., None] * v, (beta * carry)[..., None] * k], axis=-1)
    sol = jnp.einsum("nhcs,nhsv->nhcv", inverse, rhs, precision=HI)
    u, w = sol[..., :HEAD_V], sol[..., HEAD_V:]
    kw = k * decay_mat[..., -1, :, None]
    m = jnp.einsum("nhck,nhcj->nhkj", kw, w, precision=HI)
    nn = jnp.einsum("nhck,nhcv->nhkv", kw, u, precision=HI)
    a_last = carry[..., -1]
    states = [jnp.zeros((HEADS, HEAD_K, HEAD_V), jnp.float32)]
    s = nn[0]
    states.append(s)
    for c in range(1, nc - 1):
        s = a_last[c][:, None, None] * s - jnp.einsum("hkj,hjv->hkv", m[c], s, precision=HI) + nn[c]
        states.append(s)
    st = jnp.stack(states)
    p = u - jnp.einsum("nhck,nhkv->nhcv", w, st, precision=HI)
    scores = jnp.einsum("nhck,nhsk->nhcs", q, k, precision=HI) * decay_mat
    out = carry[..., None] * jnp.einsum("nhck,nhkv->nhcv", q, st, precision=HI)
    out = out + jnp.einsum("nhcs,nhsv->nhcv", scores, p, precision=HI)
    return jnp.swapaxes(out, 1, 2).reshape(length, HEADS, HEAD_V)


def mixer_core(raw_proj, gate_logits, segments, conv_weight, a_log, dt_bias):
    length = raw_proj.shape[0]
    key_dim = HEADS * HEAD_K
    conv = conv_silu(raw_proj, conv_weight, segments)
    queries = conv[:, :key_dim].reshape(length, HEADS, HEAD_K)
    keys_raw = conv[:, key_dim : 2 * key_dim].reshape(length, HEADS, HEAD_K)
    values_part = conv[:, 2 * key_dim :].reshape(length, HEADS, HEAD_V)
    queries = (
        queries
        * lax.rsqrt(jnp.sum(queries * queries, axis=-1, keepdims=True) + EPSILON)
        * HEAD_K ** (-0.5)
    )
    keys_unit = keys_raw * lax.rsqrt(jnp.sum(keys_raw * keys_raw, axis=-1, keepdims=True) + EPSILON)
    log_decay = -jnp.exp(a_log) * jax.nn.softplus(gate_logits[:, :HEADS] + dt_bias)
    write_rate = jax.nn.sigmoid(gate_logits[:, HEADS:])
    return delta_rule(queries, keys_unit, values_part, log_decay, write_rate, segments)


def out_norm(delta_out, out_gate, gain_o):
    length = delta_out.shape[0]
    gate_vals = jax.nn.silu(out_gate).reshape(length, HEADS, HEAD_V)
    normed = (
        delta_out
        * lax.rsqrt(jnp.mean(delta_out * delta_out, axis=-1, keepdims=True) + EPSILON)
        * gain_o
        * gate_vals
    )
    return normed.reshape(length, HEADS * HEAD_V)


def contract_rows(left, right):
    return lax.dot_general(
        left, right, (((0,), (0,)), ((), ())), preferred_element_type=jnp.float32
    )


def contract_cols(left, right):
    return lax.dot_general(
        left, right, (((1,), (1,)), ((), ())), preferred_element_type=jnp.float32
    )


def swiglu_grads(normed_rows, gate_pre, up_proj, grad_hidden):
    sigmoid_g = jax.nn.sigmoid(gate_pre)
    grad_gate_pre = (
        grad_hidden * up_proj * sigmoid_g * (1.0 + gate_pre * (1.0 - sigmoid_g))
    ).astype(jnp.bfloat16)
    grad_up = (grad_hidden * gate_pre * sigmoid_g).astype(jnp.bfloat16)
    grad_gate_up = jnp.stack(
        [contract_rows(normed_rows, grad_gate_pre), contract_rows(normed_rows, grad_up)]
    )
    return (grad_gate_pre, grad_up, grad_gate_up)


def per_device_body(
    tokens,
    segment_ids,
    gain_in,
    w_qkv,
    conv_w,
    w_decay,
    a_log,
    dt_bias,
    w_gate_o,
    gain_o,
    w_out,
    gain_mid,
    w_gate_up,
    w_down,
    cotangent,
):
    segments = segment_ids[0]
    residual_in = tokens.astype(jnp.float32)
    normed_f, norm_in_back = jax.vjp(rms_scale, residual_in, gain_in)
    normed_in = normed_f.astype(jnp.bfloat16)
    raw_proj = jnp.dot(normed_in, w_qkv, preferred_element_type=jnp.float32)
    gate_logits = jnp.dot(normed_in, w_decay, preferred_element_type=jnp.float32)
    out_gate = jnp.dot(normed_in, w_gate_o, preferred_element_type=jnp.float32)

    def local_core(raw_a, logit_a, conv_a, log_a, bias_a):
        return mixer_core(raw_a, logit_a, segments, conv_a, log_a, bias_a)

    delta_out, core_back = jax.vjp(local_core, raw_proj, gate_logits, conv_w, a_log, dt_bias)
    mixed_f, out_norm_back = jax.vjp(out_norm, delta_out, out_gate, gain_o)
    mixed = mixed_f.astype(jnp.bfloat16)
    stacked = jnp.concatenate([w_gate_up, w_down.T[None]], axis=0)
    stacked_rows = lax.all_gather(stacked, "row", axis=1, tiled=True)
    gate_up_rows, down_rows = stacked_rows[:2], stacked_rows[2].T
    cot_all = lax.all_gather(cotangent, "col", axis=0, tiled=True)
    mixed, gate_up_rows, down_rows, cot_all = lax.optimization_barrier(
        (mixed, gate_up_rows, down_rows, cot_all)
    )
    middle = residual_in + jnp.dot(mixed, w_out, preferred_element_type=jnp.float32)
    middle_out = lax.optimization_barrier(middle)
    normed_mf, norm_mid_back = jax.vjp(rms_scale, middle, gain_mid)
    normed_mid = normed_mf.astype(jnp.bfloat16)
    normed_all = lax.all_gather(normed_mid, "col", axis=0, tiled=True)
    gate_pre = jnp.dot(normed_all, gate_up_rows[0], preferred_element_type=jnp.float32)
    up_proj = jnp.dot(normed_all, gate_up_rows[1], preferred_element_type=jnp.float32)
    hidden = (jax.nn.silu(gate_pre) * up_proj).astype(jnp.bfloat16)
    ffn_part = jnp.dot(hidden, down_rows, preferred_element_type=jnp.float32).astype(jnp.bfloat16)
    grad_hidden = contract_cols(cot_all, down_rows)
    grad_gate_pre, grad_up, grad_gu_part = swiglu_grads(normed_all, gate_pre, up_proj, grad_hidden)
    grad_down_part = contract_rows(hidden, cot_all)
    grad_nm_part = (
        contract_cols(grad_gate_pre, gate_up_rows[0]) + contract_cols(grad_up, gate_up_rows[1])
    ).astype(jnp.bfloat16)
    grad_normed_mid = lax.psum_scatter(grad_nm_part, "col", scatter_dimension=0, tiled=True)
    grad_normed_mid = grad_normed_mid.astype(jnp.float32)
    ffn_out = lax.psum_scatter(ffn_part, "col", scatter_dimension=0, tiled=True)
    grad_gate_up, grad_down = (
        summed_by_exchange(grad_gu_part.astype(jnp.bfloat16), "row", 1),
        summed_by_exchange(grad_down_part.astype(jnp.bfloat16), "row", 1),
    )
    grad_mid_norm, grad_gain_mid = norm_mid_back(grad_normed_mid)
    grad_middle = cotangent.astype(jnp.float32) + grad_mid_norm
    grad_middle_b = grad_middle.astype(jnp.bfloat16)
    grad_out = contract_rows(mixed, grad_middle_b)
    grad_mixed = contract_cols(grad_middle_b, w_out)
    grad_delta, grad_gate_out, grad_gain_o = out_norm_back(grad_mixed)
    grad_gate_b = grad_gate_out.astype(jnp.bfloat16)
    grad_gate_o = contract_rows(normed_in, grad_gate_b)
    early_b = (grad_out.astype(jnp.bfloat16), grad_gate_o.astype(jnp.bfloat16))
    early_b, grad_delta = lax.optimization_barrier((early_b, grad_delta))
    early_b = lax.psum(early_b, ("row", "col"))
    early = [e.astype(jnp.float32) for e in early_b]
    grad_raw, grad_logits, grad_conv, grad_a_log, grad_dt_bias = core_back(grad_delta)
    grad_raw_b = grad_raw.astype(jnp.bfloat16)
    grad_logits_b = grad_logits.astype(jnp.bfloat16)
    grad_qkv = contract_rows(normed_in, grad_raw_b)
    grad_decay = contract_rows(normed_in, grad_logits_b)
    block_out = (middle_out + ffn_out.astype(jnp.float32)).astype(jnp.bfloat16)
    grad_normed_in = (
        contract_cols(grad_raw_b, w_qkv)
        + contract_cols(grad_logits_b, w_decay)
        + contract_cols(grad_gate_b, w_gate_o)
    )
    grad_in_norm, grad_gain_in = norm_in_back(grad_normed_in)
    grad_tokens = grad_middle + grad_in_norm
    qkv_b, _ = lax.optimization_barrier((grad_qkv.astype(jnp.bfloat16), early_b))
    late = [lax.psum(qkv_b, ("row", "col")).astype(jnp.float32)]
    small = summed_f32(
        (grad_gain_in, grad_conv, grad_decay, grad_a_log, grad_dt_bias, grad_gain_o, grad_gain_mid)
    )
    return (
        block_out,
        grad_tokens,
        small[0],
        late[0],
        small[1],
        small[2],
        small[3],
        small[4],
        early[1],
        small[5],
        early[0],
        small[6],
        grad_gate_up,
        grad_down,
    )


def summed_by_exchange(part, axis, dim):
    n = lax.axis_size(axis)
    shape = part.shape
    pieces = part.reshape(shape[:dim] + (n, shape[dim] // n) + shape[dim + 1 :])
    got = lax.all_to_all(pieces, axis, dim, dim, tiled=False)
    return jnp.sum(got.astype(jnp.float32), axis=dim)


def split_flat(total, parts):
    out, at = [], 0
    for p in parts:
        out.append(total[at : at + p.size].reshape(p.shape).astype(jnp.float32))
        at += p.size
    return out


def summed_f32(parts):
    flat = jnp.concatenate([p.reshape(-1) for p in parts])
    for axis in ("col", "row"):
        n = lax.axis_size(axis)
        if n & (n - 1):
            flat = lax.psum(flat, axis)
            continue
        step = 1
        while step < n:
            flat = flat + lax.ppermute(flat, axis, [(i, i ^ step) for i in range(n)])
            step *= 2
    return split_flat(flat, parts)


def solution(mesh):
    in_specs = (
        P(("row", "col"), None),
        P(("row", "col"), None),
        P(),
        P(),
        P(),
        P(),
        P(),
        P(),
        P(),
        P(),
        P(),
        P(),
        P(None, "row", "col"),
        P("col", "row"),
        P(("row", "col"), None),
    )
    out_specs = (
        P(("row", "col"), None),
        P(("row", "col"), None),
        P(),
        P(),
        P(),
        P(),
        P(),
        P(),
        P(),
        P(),
        P(),
        P(),
        P(None, "row", "col"),
        P("col", "row"),
    )
    return jax.shard_map(
        per_device_body, mesh=mesh, in_specs=in_specs, out_specs=out_specs, check_vma=False
    )
```

```python
import jax
import jax.numpy as jnp
from jax import lax
from jax.sharding import PartitionSpec as P

HEADS = 6
HEAD_K = 128
HEAD_V = 256
CONV = 4
STRETCH = 64
HI = lax.Precision.HIGHEST


EPSILON = 1e-06


def rms_scale(values, gain_vec):
    return (
        values * lax.rsqrt(jnp.mean(values * values, axis=-1, keepdims=True) + EPSILON) * gain_vec
    )


def conv_silu(raw_proj, conv_weight, segments):
    length = raw_proj.shape[0]
    mixed = raw_proj * conv_weight[CONV - 1]
    for offset in range(1, CONV):
        shifted = jnp.concatenate(
            [jnp.zeros((offset, raw_proj.shape[1]), jnp.float32), raw_proj[: length - offset]],
            axis=0,
        )
        seg_shifted = jnp.concatenate(
            [jnp.full((offset,), -1, jnp.int32), segments[: length - offset]], axis=0
        )
        keep_tap = (seg_shifted == segments).astype(jnp.float32)[:, None]
        mixed = mixed + shifted * keep_tap * conv_weight[CONV - 1 - offset]
    return jax.nn.silu(mixed)


def head_blocks(array, stretch_count):
    shaped = array.reshape((stretch_count, STRETCH) + array.shape[1:])
    return jnp.swapaxes(shaped, 1, 2)


LEAF = 8


def _mm(a, b):
    return jnp.einsum("...ij,...jk->...ik", a, b, precision=HI)


def _unit_lower_inverse_fwd_impl(strict_part):
    n = strict_part.shape[-1]
    nb = n // LEAF
    eye = jnp.eye(LEAF, dtype=strict_part.dtype)
    diag = jnp.stack(
        [strict_part[..., i * LEAF:(i + 1) * LEAF, i * LEAF:(i + 1) * LEAF] for i in range(nb)], axis=-3
    )
    sq = _mm(diag, diag)
    blocks = _mm(_mm(eye - diag, eye + sq), eye + _mm(sq, sq))
    size = LEAF
    while size < n:
        count = n // (2 * size)
        upper_inv = blocks[..., 0::2, :, :]
        lower_inv = blocks[..., 1::2, :, :]
        cross = jnp.stack(
            [strict_part[..., (2 * p + 1) * size:(2 * p + 2) * size, 2 * p * size:(2 * p + 1) * size] for p in range(count)],
            axis=-3,
        )
        corner = -_mm(lower_inv, _mm(cross, upper_inv))
        zeros = jnp.zeros_like(corner)
        top = jnp.concatenate([upper_inv, zeros], axis=-1)
        bottom = jnp.concatenate([corner, lower_inv], axis=-1)
        blocks = jnp.concatenate([top, bottom], axis=-2)
        size *= 2
    return blocks[..., 0, :, :]


@jax.custom_vjp
def unit_lower_inverse(strict_part):
    return _unit_lower_inverse_fwd_impl(strict_part)


def _uli_fwd(strict_part):
    inv = _unit_lower_inverse_fwd_impl(strict_part)
    return inv, inv


def _uli_bwd(inv, grad):
    n = inv.shape[-1]
    below = jnp.arange(n)[:, None] > jnp.arange(n)[None, :]
    inv_t = jnp.swapaxes(inv, -1, -2)
    return (jnp.where(below, -_mm(inv_t, _mm(grad, inv_t)), 0.0),)


unit_lower_inverse.defvjp(_uli_fwd, _uli_bwd)


def delta_rule(queries, keys_unit, values_part, log_decay, write_rate, segments):
    length = queries.shape[0]
    nc = length // STRETCH
    q = head_blocks(queries, nc)
    k = head_blocks(keys_unit, nc)
    v = head_blocks(values_part, nc)
    g = head_blocks(log_decay, nc)
    beta = head_blocks(write_rate, nc)
    seg = segments.reshape(nc, STRETCH)
    seg_prev = jnp.concatenate([jnp.full((1,), -1, jnp.int32), seg[:-1, -1]], axis=0)
    row = jnp.arange(STRETCH)[:, None]
    col = jnp.arange(STRETCH)[None, :]
    cum = jnp.cumsum(g, axis=-1)
    live = ((seg[:, :, None] == seg[:, None, :]) & (row >= col))[:, None]
    gap = cum[..., :, None] - cum[..., None, :]
    decay_mat = jnp.where(live, jnp.exp(jnp.where(live, gap, 0.0)), 0.0)
    carry = jnp.exp(cum) * (seg == seg_prev[:, None]).astype(jnp.float32)[:, None, :]
    gram = jnp.einsum("nhck,nhsk->nhcs", k, k, precision=HI)
    strict = jnp.where((row > col)[None, None], decay_mat, 0.0)
    inverse = unit_lower_inverse(beta[..., None] * strict * gram)
    rhs = jnp.concatenate([beta[..., None] * v, (beta * carry)[..., None] * k], axis=-1)
    sol = jnp.einsum("nhcs,nhsv->nhcv", inverse, rhs, precision=HI)
    u, w = sol[..., :HEAD_V], sol[..., HEAD_V:]
    kw = k * decay_mat[..., -1, :, None]
    m = jnp.einsum("nhck,nhcj->nhkj", kw, w, precision=HI)
    nn = jnp.einsum("nhck,nhcv->nhkv", kw, u, precision=HI)
    a_last = carry[..., -1]
    states = [jnp.zeros((HEADS, HEAD_K, HEAD_V), jnp.float32)]
    s = nn[0]
    states.append(s)
    for c in range(1, nc - 1):
        s = a_last[c][:, None, None] * s - jnp.einsum("hkj,hjv->hkv", m[c], s, precision=HI) + nn[c]
        states.append(s)
    st = jnp.stack(states)
    p = u - jnp.einsum("nhck,nhkv->nhcv", w, st, precision=HI)
    scores = jnp.einsum("nhck,nhsk->nhcs", q, k, precision=HI) * decay_mat
    out = carry[..., None] * jnp.einsum("nhck,nhkv->nhcv", q, st, precision=HI)
    out = out + jnp.einsum("nhcs,nhsv->nhcv", scores, p, precision=HI)
    return jnp.swapaxes(out, 1, 2).reshape(length, HEADS, HEAD_V)


def mixer_core(raw_proj, gate_logits, segments, conv_weight, a_log, dt_bias):
    length = raw_proj.shape[0]
    key_dim = HEADS * HEAD_K
    conv = conv_silu(raw_proj, conv_weight, segments)
    queries = conv[:, :key_dim].reshape(length, HEADS, HEAD_K)
    keys_raw = conv[:, key_dim : 2 * key_dim].reshape(length, HEADS, HEAD_K)
    values_part = conv[:, 2 * key_dim :].reshape(length, HEADS, HEAD_V)
    queries = (
        queries
        * lax.rsqrt(jnp.sum(queries * queries, axis=-1, keepdims=True) + EPSILON)
        * HEAD_K ** (-0.5)
    )
    keys_unit = keys_raw * lax.rsqrt(jnp.sum(keys_raw * keys_raw, axis=-1, keepdims=True) + EPSILON)
    log_decay = -jnp.exp(a_log) * jax.nn.softplus(gate_logits[:, :HEADS] + dt_bias)
    write_rate = jax.nn.sigmoid(gate_logits[:, HEADS:])
    return delta_rule(queries, keys_unit, values_part, log_decay, write_rate, segments)


def out_norm(delta_out, out_gate, gain_o):
    length = delta_out.shape[0]
    gate_vals = jax.nn.silu(out_gate).reshape(length, HEADS, HEAD_V)
    normed = (
        delta_out
        * lax.rsqrt(jnp.mean(delta_out * delta_out, axis=-1, keepdims=True) + EPSILON)
        * gain_o
        * gate_vals
    )
    return normed.reshape(length, HEADS * HEAD_V)


def contract_rows(left, right):
    return lax.dot_general(
        left, right, (((0,), (0,)), ((), ())), preferred_element_type=jnp.float32
    )


def contract_cols(left, right):
    return lax.dot_general(
        left, right, (((1,), (1,)), ((), ())), preferred_element_type=jnp.float32
    )


def swiglu_grads(normed_rows, gate_pre, up_proj, grad_hidden):
    sigmoid_g = jax.nn.sigmoid(gate_pre)
    grad_gate_pre = (
        grad_hidden * up_proj * sigmoid_g * (1.0 + gate_pre * (1.0 - sigmoid_g))
    ).astype(jnp.bfloat16)
    grad_up = (grad_hidden * gate_pre * sigmoid_g).astype(jnp.bfloat16)
    grad_gate_up = jnp.stack(
        [contract_rows(normed_rows, grad_gate_pre), contract_rows(normed_rows, grad_up)]
    )
    return (grad_gate_pre, grad_up, grad_gate_up)


def per_device_body(
    tokens,
    segment_ids,
    gain_in,
    w_qkv,
    conv_w,
    w_decay,
    a_log,
    dt_bias,
    w_gate_o,
    gain_o,
    w_out,
    gain_mid,
    w_gate_up,
    w_down,
    cotangent,
):
    segments = segment_ids[0]
    residual_in = tokens.astype(jnp.float32)
    normed_f, norm_in_back = jax.vjp(rms_scale, residual_in, gain_in)
    normed_in = normed_f.astype(jnp.bfloat16)
    raw_proj = jnp.dot(normed_in, w_qkv, preferred_element_type=jnp.float32)
    gate_logits = jnp.dot(normed_in, w_decay, preferred_element_type=jnp.float32)
    out_gate = jnp.dot(normed_in, w_gate_o, preferred_element_type=jnp.float32)

    def local_core(raw_a, logit_a, conv_a, log_a, bias_a):
        return mixer_core(raw_a, logit_a, segments, conv_a, log_a, bias_a)

    delta_out, core_back = jax.vjp(local_core, raw_proj, gate_logits, conv_w, a_log, dt_bias)
    mixed_f, out_norm_back = jax.vjp(out_norm, delta_out, out_gate, gain_o)
    mixed = mixed_f.astype(jnp.bfloat16)
    stacked = jnp.concatenate([w_gate_up, w_down.T[None]], axis=0)
    stacked_rows = lax.all_gather(stacked, "row", axis=1, tiled=True)
    gate_up_rows, down_rows = stacked_rows[:2], stacked_rows[2].T
    cot_all = lax.all_gather(cotangent, "col", axis=0, tiled=True)
    mixed, gate_up_rows, down_rows, cot_all = lax.optimization_barrier(
        (mixed, gate_up_rows, down_rows, cot_all)
    )
    middle = residual_in + jnp.dot(mixed, w_out, preferred_element_type=jnp.float32)
    middle_out = lax.optimization_barrier(middle)
    normed_mf, norm_mid_back = jax.vjp(rms_scale, middle, gain_mid)
    normed_mid = normed_mf.astype(jnp.bfloat16)
    normed_all = lax.all_gather(normed_mid, "col", axis=0, tiled=True)
    gate_pre = jnp.dot(normed_all, gate_up_rows[0], preferred_element_type=jnp.float32)
    up_proj = jnp.dot(normed_all, gate_up_rows[1], preferred_element_type=jnp.float32)
    hidden = (jax.nn.silu(gate_pre) * up_proj).astype(jnp.bfloat16)
    ffn_part = jnp.dot(hidden, down_rows, preferred_element_type=jnp.float32).astype(jnp.bfloat16)
    grad_hidden = contract_cols(cot_all, down_rows)
    grad_gate_pre, grad_up, grad_gu_part = swiglu_grads(normed_all, gate_pre, up_proj, grad_hidden)
    grad_down_part = contract_rows(hidden, cot_all)
    grad_nm_part = (
        contract_cols(grad_gate_pre, gate_up_rows[0]) + contract_cols(grad_up, gate_up_rows[1])
    ).astype(jnp.bfloat16)
    grad_normed_mid = lax.psum_scatter(grad_nm_part, "col", scatter_dimension=0, tiled=True)
    grad_normed_mid = grad_normed_mid.astype(jnp.float32)
    ffn_out = summed_by_exchange(ffn_part, "col", 0)
    grad_gate_up, grad_down = (
        summed_by_exchange(grad_gu_part.astype(jnp.bfloat16), "row", 1),
        summed_by_exchange(grad_down_part.astype(jnp.bfloat16), "row", 1),
    )
    grad_mid_norm, grad_gain_mid = norm_mid_back(grad_normed_mid)
    grad_middle = cotangent.astype(jnp.float32) + grad_mid_norm
    grad_middle_b = grad_middle.astype(jnp.bfloat16)
    grad_out = contract_rows(mixed, grad_middle_b)
    grad_mixed = contract_cols(grad_middle_b, w_out)
    grad_delta, grad_gate_out, grad_gain_o = out_norm_back(grad_mixed)
    grad_gate_b = grad_gate_out.astype(jnp.bfloat16)
    grad_gate_o_t = contract_rows(grad_gate_b, normed_in)
    early_b = jnp.concatenate(
        [grad_out.astype(jnp.bfloat16), grad_gate_o_t.astype(jnp.bfloat16)], axis=0
    )
    early_b, grad_delta = lax.optimization_barrier((early_b, grad_delta))
    early_b = lax.psum(early_b, ("row", "col"))
    rows_out = grad_out.shape[0]
    early = [early_b[:rows_out].astype(jnp.float32), early_b[rows_out:].T.astype(jnp.float32)]
    grad_raw, grad_logits, grad_conv, grad_a_log, grad_dt_bias = core_back(grad_delta)
    grad_raw_b = grad_raw.astype(jnp.bfloat16)
    grad_logits_b = grad_logits.astype(jnp.bfloat16)
    grad_qkv = contract_rows(normed_in, grad_raw_b)
    grad_decay = contract_rows(normed_in, grad_logits_b)
    block_out = (middle_out + ffn_out).astype(jnp.bfloat16)
    grad_normed_in = (
        contract_cols(grad_raw_b, w_qkv)
        + contract_cols(grad_logits_b, w_decay)
        + contract_cols(grad_gate_b, w_gate_o)
    )
    grad_in_norm, grad_gain_in = norm_in_back(grad_normed_in)
    grad_tokens = grad_middle + grad_in_norm
    qkv_b, _ = lax.optimization_barrier((grad_qkv.astype(jnp.bfloat16), early_b))
    late = [lax.psum(qkv_b, ("row", "col")).astype(jnp.float32)]
    small = summed_f32(
        (grad_gain_in, grad_conv, grad_decay, grad_a_log, grad_dt_bias, grad_gain_o, grad_gain_mid)
    )
    return (
        block_out,
        grad_tokens,
        small[0],
        late[0],
        small[1],
        small[2],
        small[3],
        small[4],
        early[1],
        small[5],
        early[0],
        small[6],
        grad_gate_up,
        grad_down,
    )


def summed_by_exchange(part, axis, dim):
    n = lax.axis_size(axis)
    shape = part.shape
    pieces = part.reshape(shape[:dim] + (n, shape[dim] // n) + shape[dim + 1 :])
    got = lax.all_to_all(pieces, axis, dim, dim, tiled=False)
    return jnp.sum(got.astype(jnp.float32), axis=dim)


def split_flat(total, parts):
    out, at = [], 0
    for p in parts:
        out.append(total[at : at + p.size].reshape(p.shape).astype(jnp.float32))
        at += p.size
    return out


def summed_f32(parts):
    flat = jnp.concatenate([p.reshape(-1) for p in parts])
    for axis in ("col", "row"):
        n = lax.axis_size(axis)
        if n & (n - 1):
            flat = lax.psum(flat, axis)
            continue
        step = 1
        while step < n:
            flat = flat + lax.ppermute(flat, axis, [(i, i ^ step) for i in range(n)])
            step *= 2
    return split_flat(flat, parts)


def solution(mesh):
    in_specs = (
        P(("row", "col"), None),
        P(("row", "col"), None),
        P(),
        P(),
        P(),
        P(),
        P(),
        P(),
        P(),
        P(),
        P(),
        P(),
        P(None, "row", "col"),
        P("col", "row"),
        P(("row", "col"), None),
    )
    out_specs = (
        P(("row", "col"), None),
        P(("row", "col"), None),
        P(),
        P(),
        P(),
        P(),
        P(),
        P(),
        P(),
        P(),
        P(),
        P(),
        P(None, "row", "col"),
        P("col", "row"),
    )
    return jax.shard_map(
        per_device_body, mesh=mesh, in_specs=in_specs, out_specs=out_specs, check_vma=False
    )
```
